32 devices in a mesh: grp: 2 (over y), tm: 8 (over z, x), rows: 1, chan: 2 (over core).
Axes of the slice: x: 2, y: 2, z: 4, core: 2. Of those that a mesh axis runs over, the one named last changes fastest.
Arguments:
- frames_in: bfloat16 [64, 1, 64, 512], P(('grp', 'tm'), 'rows'), parts along dimension 0, may hold values from -6 to 6
- in_kernel: bfloat16 [3, 3, 512, 512], P(None, None, None, 'chan'), may hold values from -0.09375 to 0.09375
- out_kernel: bfloat16 [3, 3, 512, 512], P(None, None, 'chan'), may hold values from -0.09375 to 0.09375
- decay_rate: float32 [512], P('chan'), may hold values from 0 to 1, as said below
- frame_keep: float32 [64], P('grp'), parts along dimension 0, may hold values from 0.5 to 1
- out_grad: bfloat16 [64, 1, 64, 512], P(('grp', 'tm'), 'rows'), parts along dimension 0, may hold values from -6 to 6
Outputs:
- mixed: bfloat16 [64, 1, 64, 512], P(('grp', 'tm'), 'rows', None, 'chan'), parts along dimension 0
- grad_in: bfloat16 [64, 1, 64, 512], P(('grp', 'tm'), 'rows', None, 'chan'), parts along dimension 0
- grad_decay: float32 [1024], P(('grp', 'chan')), parts along dimension 0
The draws below stay inside these ranges and needn't reach their ends.
There are 2 independent parts, one for each index of `grp`. The reference program is written for one: setup_inputs(seed, part) draws one part's arguments, and reference() takes and returns one part's arrays. A program takes and returns all parts, laid end to end along the dimension named above; an argument that names none is the same for every part. Nothing has to cross between parts.
Inputs may be any that keep to these rules, and one draw needn't show every extreme that they name: `decay_rate`: every decay factor lies strictly between the bounds.
All inputs are finite; a program needn't handle non-finite values.
Results may differ from the reference program's by a relative error of at most 0.009.
Values may be sent and summed in bfloat16 or wider, within the bound.
No kernel may reach another device: no remote copies, remote signals or barrier semaphores. Data moves between devices by JAX's collectives and lax.ppermute only.
A program may use at most 64 MiB of HBM per device.

```python
import jax
import jax.numpy as jnp
from jax import lax

H = 512
P_SIZE = 512
COLS = 64
ROWS = 1
FRAMES = 32


def draw_decay_rate(key, part):
    key_slow, key_span = jax.random.split(jax.random.fold_in(key, 11), 2)
    slow_share = 0.5
    slowness = jax.random.bernoulli(key_slow, slow_share, (P_SIZE,))
    spread = jax.random.uniform(key_span, (P_SIZE,), jnp.float32)
    slow_span = FRAMES * jnp.exp(spread * jnp.log(4.0))
    fast_span = FRAMES / 16.0 * jnp.exp(spread * jnp.log(4.0))
    span = jnp.where(slowness, slow_span, fast_span)
    return jnp.exp(-1.0 / span).astype(jnp.float32)


def draw_frame_keep(key, part):
    key_where, key_level = jax.random.split(jax.random.fold_in(key, 23), 2)
    chosen = jax.random.permutation(key_where, FRAMES)[:3]
    levels = jax.random.uniform(key_level, (3,), jnp.float32, 0.5, 0.8)
    return jnp.ones((FRAMES,), jnp.float32).at[chosen].set(levels)


def level_of(rng, dims, pieces, smallest, high):
    def one(position, shards_of):
        draws = jax.random.uniform(jax.random.fold_in(jax.random.fold_in(rng, 6), position), (shards_of,), jnp.float32, smallest / len(pieces), high / len(pieces))
        return jnp.repeat(jnp.exp(draws), dims[position] // shards_of).reshape((-1,) + (1,) * (len(dims) - position - 1))

    level = one(*pieces[0])
    for cut in pieces[1:]:
        level = level * one(*cut)
    return level


def gaussian(key, extent, scale, reach, pieces=(), held_as=jnp.bfloat16):
    loudness = level_of(key, extent, pieces, -0.22, 0.18) if pieces else 1.0
    array = jax.random.normal(key, extent, jnp.float32) * scale * loudness
    return jnp.minimum(jnp.maximum(array, -reach), reach).astype(held_as)


def setup_inputs(seed: int = 0, part: int = 0) -> dict:
    keys = jax.random.split(jax.random.key(seed), 7)
    part_splits = jax.random.split(jax.random.fold_in(keys[6], part), 7)
    return {
        "frames_in": gaussian(part_splits[0], (FRAMES, ROWS, COLS, H), 1.0, 6.0, ((0, 8),)),
        "in_kernel": gaussian(keys[1], (3, 3, H, P_SIZE), (9 * H) ** -0.5, 0.09375, ((3, 2),)),
        "out_kernel": gaussian(keys[2], (3, 3, P_SIZE, H), (9 * P_SIZE) ** -0.5, 0.09375, ((2, 2),)),
        "decay_rate": draw_decay_rate(jax.random.fold_in(keys[6], 71), part),
        "frame_keep": draw_frame_keep(jax.random.fold_in(jax.random.fold_in(keys[6], part), 71), part),
        "out_grad": gaussian(part_splits[5], (FRAMES, ROWS, COLS, H), 1.0, 6.0, ((0, 8),)),
    }


def conv_apply(extended, kernel, transpose):
    padded = jnp.pad(extended, ((0, 0), (0, 0), (1, 1), (0, 0)))
    frame_count = extended.shape[0]
    row_count = extended.shape[1] - 2
    col_count = extended.shape[2]
    channels = extended.shape[3]
    summed = None
    for row_tap in range(3):
        for col_tap in range(3):
            if transpose:
                portion = padded[:, 2 - row_tap:2 - row_tap + row_count, 2 - col_tap:2 - col_tap + col_count, :]
                term = lax.dot_general(portion.reshape(-1, channels), kernel[row_tap, col_tap], (((1,), (1,)), ((), ())), preferred_element_type=jnp.float32)
            else:
                portion = padded[:, row_tap:row_tap + row_count, col_tap:col_tap + col_count, :]
                term = jnp.dot(portion.reshape(-1, channels), kernel[row_tap, col_tap], preferred_element_type=jnp.float32)
            summed = term if summed is None else summed + term
    return summed.reshape(frame_count, row_count, col_count, -1)

def pad_rows(field):
    return jnp.pad(field, ((0, 0), (1, 1), (0, 0), (0, 0)))

def reference(frames_in, in_kernel, out_kernel, decay_rate, frame_keep, out_grad):
    rates = decay_rate
    input_gain = jnp.sqrt(1.0 - rates * rates)
    values = conv_apply(pad_rows(frames_in), in_kernel, False)
    decays = frame_keep[:, None] * rates[None, :]

    def forward_step(running, inputs):
        factor, current = inputs
        running = factor * running + input_gain * current
        return (running, running)
    start_state = jnp.zeros(values.shape[1:], jnp.float32)
    _, states = lax.scan(forward_step, start_state, (decays, values))
    previous = jnp.concatenate([start_state[None], states[:-1]], axis=0)
    mixed = conv_apply(pad_rows(states.astype(jnp.bfloat16)), out_kernel, False).astype(jnp.bfloat16)
    adjoint_in = conv_apply(pad_rows(out_grad), out_kernel, True)
    decays_next = jnp.concatenate([decays[1:], jnp.zeros((1, decays.shape[1]), jnp.float32)], axis=0)

    def backward_step(running, inputs):
        factor, current = inputs
        running = current + factor * running
        return (running, running)
    _, adjoints = lax.scan(backward_step, start_state, (decays_next, adjoint_in), reverse=True)
    grad_in = conv_apply(pad_rows(adjoints.astype(jnp.bfloat16)), in_kernel, True).astype(jnp.bfloat16)
    terms = adjoints * (decays[:, None, None, :] * previous - rates * rates / input_gain * values)
    total_count = values.shape[0] * values.shape[1] * values.shape[2]
    grad_decay = lax.optimization_barrier(jnp.sum(terms, axis=(0, 1, 2))) / jnp.sqrt(jnp.float32(total_count))
    return (mixed, grad_in, grad_decay)
```

```python
import math

import jax
import jax.numpy as jnp
from jax import lax
from jax.sharding import PartitionSpec as P


def row_halo(cells):
    count = lax.axis_size("rows")
    if count == 1:
        return None
    ends = count - 1
    head = cells[:, :1]
    tail = cells[:, -1:]
    top = lax.ppermute(tail, "rows", [(i, i + 1) for i in range(ends)])
    bottom = lax.ppermute(head, "rows", [(i + 1, i) for i in range(ends)])
    return top, bottom


def conv_apply(cells, halo, kernel, transpose):
    frame_count, row_count, col_count, channels = cells.shape
    if halo is None and row_count == 1:
        row_taps = (1,)
        extended = cells
    else:
        if halo is None:
            zero = jnp.zeros_like(cells[:, :1])
            halo = (zero, zero)
        row_taps = (0, 1, 2)
        extended = jnp.concatenate([halo[0], cells, halo[1]], axis=1)
    if len(row_taps) == 1:
        extended = jnp.pad(extended, ((0, 0), (1, 1), (0, 0), (0, 0)))
    padded = jnp.pad(extended, ((0, 0), (0, 0), (1, 1), (0, 0)))
    summed = None
    for row_tap in row_taps:
        for col_tap in range(3):
            if transpose:
                portion = padded[
                    :,
                    2 - row_tap : 2 - row_tap + row_count,
                    2 - col_tap : 2 - col_tap + col_count,
                    :,
                ]
                term = lax.dot_general(
                    portion.reshape(-1, channels),
                    kernel[row_tap, col_tap],
                    (((1,), (1,)), ((), ())),
                    preferred_element_type=jnp.float32,
                )
            else:
                portion = padded[:, row_tap : row_tap + row_count, col_tap : col_tap + col_count, :]
                term = jnp.dot(
                    portion.reshape(-1, channels),
                    kernel[row_tap, col_tap],
                    preferred_element_type=jnp.float32,
                )
            summed = term if summed is None else summed + term
    return summed.reshape(frame_count, row_count, col_count, -1)


def combine_packed(earlier, later):
    is_state = lax.broadcasted_iota(jnp.int32, later.shape, 0) > 0
    return later[0:1] * earlier + jnp.where(is_state, later, 0.0)


def exclusive_scan(packed, axis, reverse):
    count = lax.axis_size(axis)
    mine = lax.axis_index(axis)
    rank = count - 1 - mine if reverse else mine
    is_state = lax.broadcasted_iota(jnp.int32, packed.shape, 0) > 0
    excl = jnp.where(is_state, 0.0, 1.0).astype(packed.dtype)
    incl = packed
    step = 1
    while step < count:
        if reverse:
            pairs = [(i, i - step) for i in range(step, count)]
        else:
            pairs = [(i, i + step) for i in range(count - step)]
        got = lax.ppermute(incl, axis, pairs)
        has = rank >= step
        excl = jnp.where(has, combine_packed(got, excl), excl)
        if 2 * step < count:
            incl = jnp.where(has, combine_packed(got, incl), incl)
        step *= 2
    return excl


def all_sum(value, axis):
    count = lax.axis_size(axis)
    if count == 1:
        return value
    if count & (count - 1) == 0:
        step = 1
        while step < count:
            value = value + lax.ppermute(value, axis, [(i, i ^ step) for i in range(count)])
            step *= 2
        return value
    return lax.psum(value, axis)


def chan_sum(cells, halo, kernel, transpose, out_axis_kernel):
    count = lax.axis_size("chan")
    mine = lax.axis_index("chan")
    width = kernel.shape[out_axis_kernel] // count
    if count != 2:
        part = conv_apply(cells, halo, kernel, transpose)
        return lax.psum_scatter(part.astype(jnp.bfloat16), "chan", scatter_dimension=3, tiled=True)
    other_kernel = lax.dynamic_slice_in_dim(kernel, (1 - mine) * width, width, axis=out_axis_kernel)
    own_kernel = lax.dynamic_slice_in_dim(kernel, mine * width, width, axis=out_axis_kernel)
    other = conv_apply(cells, halo, other_kernel, transpose).astype(jnp.bfloat16)
    got = lax.ppermute(other, "chan", [(0, 1), (1, 0)])
    own = conv_apply(cells, halo, own_kernel, transpose)
    return (own + got.astype(jnp.float32)).astype(jnp.bfloat16)


def local(frames_in, in_kernel, out_kernel, decay_rate, frame_keep, out_grad):
    frame_count, row_count, col_count = frames_in.shape[:3]
    channels = decay_rate.shape[0]
    position = lax.axis_index("tm")
    blocks = lax.axis_size("tm")
    values = conv_apply(frames_in, row_halo(frames_in), in_kernel, False)
    adjoint_in = conv_apply(out_grad, row_halo(out_grad), out_kernel, True)
    input_gain = jnp.sqrt(1.0 - decay_rate * decay_rate)
    keep_padded = jnp.concatenate([frame_keep, jnp.zeros((1,), jnp.float32)])
    offset = position * frame_count
    keep_here = lax.dynamic_slice_in_dim(keep_padded, offset, frame_count)
    keep_next = lax.dynamic_slice_in_dim(keep_padded, offset + 1, frame_count)
    decays = keep_here[:, None] * decay_rate[None, :]
    decays_next = keep_next[:, None] * decay_rate[None, :]

    running = None
    product = None
    local_states, products = [], []
    for t in range(frame_count):
        fresh = input_gain * values[t]
        running = fresh if running is None else decays[t] * running + fresh
        product = decays[t] if product is None else product * decays[t]
        local_states.append(running)
        products.append(product)
    running = None
    product = None
    back_states, back_products = [None] * frame_count, [None] * frame_count
    for t in reversed(range(frame_count)):
        running = adjoint_in[t] if running is None else adjoint_in[t] + decays_next[t] * running
        product = decays_next[t] if product is None else product * decays_next[t]
        back_states[t] = running
        back_products[t] = product

    cells = row_count * col_count

    def pack(prod, state):
        return jnp.concatenate([prod[None, :], state.reshape(cells, channels)], axis=0)

    carry_in = exclusive_scan(pack(products[-1], local_states[-1]), "tm", False)[1:]
    carry_back = exclusive_scan(pack(back_products[0], back_states[0]), "tm", True)[1:]
    carry_in = carry_in.reshape(row_count, col_count, channels)
    carry_back = carry_back.reshape(row_count, col_count, channels)

    states = jnp.stack([local_states[t] + products[t] * carry_in for t in range(frame_count)])
    adjoints = jnp.stack([back_states[t] + back_products[t] * carry_back for t in range(frame_count)])
    previous = jnp.concatenate([carry_in[None], states[:-1]], axis=0)
    terms = adjoints * (
        decays[:, None, None, :] * previous - decay_rate * decay_rate / input_gain * values
    )
    total_count = frame_count * blocks * row_count * lax.axis_size("rows") * col_count
    grad_decay = all_sum(all_sum(jnp.sum(terms, axis=(0, 1, 2)), "tm"), "rows") / math.sqrt(total_count)

    state_b = states.astype(jnp.bfloat16)
    adjoint_b = adjoints.astype(jnp.bfloat16)
    mixed = chan_sum(state_b, row_halo(state_b), out_kernel, False, 3)
    grad_in = chan_sum(adjoint_b, row_halo(adjoint_b), in_kernel, True, 2)
    return (mixed, grad_in, grad_decay)


def solution(mesh):
    placed = (
        P(("grp", "tm"), "rows", None, None),
        P(None, None, None, "chan"),
        P(None, None, "chan", None),
        P("chan"),
        P("grp"),
        P(("grp", "tm"), "rows", None, None),
    )
    return jax.shard_map(
        local,
        mesh=mesh,
        in_specs=placed,
        out_specs=(
            P(("grp", "tm"), "rows", None, "chan"),
            P(("grp", "tm"), "rows", None, "chan"),
            P(("grp", "chan")),
        ),
        check_vma=False,
    )
```

```python
import math

import jax
import jax.numpy as jnp
from jax import lax
from jax.sharding import PartitionSpec as P


def row_halo(cells):
    count = lax.axis_size("rows")
    if count == 1:
        return None
    ends = count - 1
    head = cells[:, :1]
    tail = cells[:, -1:]
    top = lax.ppermute(tail, "rows", [(i, i + 1) for i in range(ends)])
    bottom = lax.ppermute(head, "rows", [(i + 1, i) for i in range(ends)])
    return top, bottom


def row_taps_of(halo, row_count):
    return (1,) if halo is None and row_count == 1 else (0, 1, 2)


def prep_kernel(kernel, transpose, row_taps):
    if transpose:
        flipped = kernel[::-1, ::-1]
        taps = jnp.stack([flipped[a] for a in row_taps])
        taps = jnp.swapaxes(taps, 2, 3)
    else:
        taps = jnp.stack([kernel[a] for a in row_taps])
    return lax.optimization_barrier(taps)


def conv_apply(cells, halo, taps, row_taps):
    frame_count, row_count, col_count, channels = cells.shape
    if len(row_taps) == 1:
        extended = jnp.pad(cells, ((0, 0), (1, 1), (0, 0), (0, 0)))
    else:
        if halo is None:
            zero = jnp.zeros_like(cells[:, :1])
            halo = (zero, zero)
        extended = jnp.concatenate([halo[0], cells, halo[1]], axis=1)
    padded = jnp.pad(extended, ((0, 0), (0, 0), (1, 1), (0, 0)))
    summed = None
    for index, row_tap in enumerate(row_taps):
        for col_tap in range(3):
            portion = padded[:, row_tap : row_tap + row_count, col_tap : col_tap + col_count, :]
            term = jnp.dot(
                portion.reshape(-1, channels),
                taps[index, col_tap],
                preferred_element_type=jnp.float32,
            )
            summed = term if summed is None else summed + term
    return summed.reshape(frame_count, row_count, col_count, -1)


def all_sum(value, axis):
    count = lax.axis_size(axis)
    if count == 1:
        return value
    if count & (count - 1) == 0:
        step = 1
        while step < count:
            value = value + lax.ppermute(value, axis, [(i, i ^ step) for i in range(count)])
            step *= 2
        return value
    return lax.psum(value, axis)


def chan_sum(cells, halo, taps, row_taps):
    count = lax.axis_size("chan")
    mine = lax.axis_index("chan")
    width = taps.shape[3] // count
    if count != 2:
        part = conv_apply(cells, halo, taps, row_taps)
        return lax.psum_scatter(part.astype(jnp.bfloat16), "chan", scatter_dimension=3, tiled=True)
    other_taps = lax.dynamic_slice_in_dim(taps, (1 - mine) * width, width, axis=3)
    own_taps = lax.dynamic_slice_in_dim(taps, mine * width, width, axis=3)
    other = conv_apply(cells, halo, other_taps, row_taps).astype(jnp.bfloat16)
    got = lax.ppermute(other, "chan", [(0, 1), (1, 0)])
    own = conv_apply(cells, halo, own_taps, row_taps)
    return (own + got.astype(jnp.float32)).astype(jnp.bfloat16)


def block_carries(fwd_end, bwd_start, fwd_prod, bwd_prod, axis):
    count = lax.axis_size(axis)
    mine = lax.axis_index(axis)
    received = {}
    for step in range(1, count):
        message = jnp.where(mine + step < count, fwd_end, bwd_start)
        received[step] = lax.ppermute(message, axis, [(i, (i + step) % count) for i in range(count)])
    carry_in = jnp.zeros_like(fwd_end)
    for step in reversed(range(1, count)):
        source = mine - step
        factor = lax.dynamic_index_in_dim(fwd_prod, jnp.maximum(source, 0), 0, keepdims=False)
        carry_in = jnp.where(source >= 0, received[step], 0.0) + factor * carry_in
    carry_back = jnp.zeros_like(bwd_start)
    for step in reversed(range(1, count)):
        source = mine + step
        factor = lax.dynamic_index_in_dim(bwd_prod, jnp.minimum(source, count - 1), 0, keepdims=False)
        carry_back = jnp.where(source < count, received[count - step], 0.0) + factor * carry_back
    return carry_in, carry_back


def local(frames_in, in_kernel, out_kernel, decay_rate, frame_keep, out_grad):
    frame_count, row_count, col_count = frames_in.shape[:3]
    position = lax.axis_index("tm")
    blocks = lax.axis_size("tm")
    in_halo = row_halo(frames_in)
    grad_halo = row_halo(out_grad)
    row_taps = row_taps_of(in_halo, row_count)
    values = conv_apply(frames_in, in_halo, prep_kernel(in_kernel, False, row_taps), row_taps)
    adjoint_in = conv_apply(out_grad, grad_halo, prep_kernel(out_kernel, True, row_taps), row_taps)
    input_gain = jnp.sqrt(1.0 - decay_rate * decay_rate)
    keep_padded = jnp.concatenate([frame_keep, jnp.zeros((1,), jnp.float32)])
    offset = position * frame_count
    keep_here = lax.dynamic_slice_in_dim(keep_padded, offset, frame_count)
    keep_next = lax.dynamic_slice_in_dim(keep_padded, offset + 1, frame_count)
    decays = keep_here[:, None] * decay_rate[None, :]
    decays_next = keep_next[:, None] * decay_rate[None, :]

    running = None
    product = None
    local_states, products = [], []
    for t in range(frame_count):
        fresh = input_gain * values[t]
        running = fresh if running is None else decays[t] * running + fresh
        product = decays[t] if product is None else product * decays[t]
        local_states.append(running)
        products.append(product)
    running = None
    product = None
    back_states, back_products = [None] * frame_count, [None] * frame_count
    for t in reversed(range(frame_count)):
        running = adjoint_in[t] if running is None else adjoint_in[t] + decays_next[t] * running
        product = decays_next[t] if product is None else product * decays_next[t]
        back_states[t] = running
        back_products[t] = product

    all_decays = (frame_keep[:, None] * decay_rate[None, :]).reshape(blocks, frame_count, -1)
    all_next = (keep_padded[1:, None] * decay_rate[None, :]).reshape(blocks, frame_count, -1)
    fwd_prod = all_decays[:, 0]
    for t in range(1, frame_count):
        fwd_prod = fwd_prod * all_decays[:, t]
    bwd_prod = all_next[:, frame_count - 1]
    for t in reversed(range(frame_count - 1)):
        bwd_prod = bwd_prod * all_next[:, t]
    carry_in, carry_back = block_carries(local_states[-1], back_states[0], fwd_prod, bwd_prod, "tm")

    states = jnp.stack([local_states[t] + products[t] * carry_in for t in range(frame_count)])
    adjoints = jnp.stack([back_states[t] + back_products[t] * carry_back for t in range(frame_count)])
    previous = jnp.concatenate([carry_in[None], states[:-1]], axis=0)
    terms = adjoints * (
        decays[:, None, None, :] * previous - decay_rate * decay_rate / input_gain * values
    )
    total_count = frame_count * blocks * row_count * lax.axis_size("rows") * col_count
    grad_decay = all_sum(all_sum(jnp.sum(terms, axis=(0, 1, 2)), "tm"), "rows") / math.sqrt(total_count)

    state_b = states.astype(jnp.bfloat16)
    adjoint_b = adjoints.astype(jnp.bfloat16)
    mixed = chan_sum(state_b, row_halo(state_b), prep_kernel(out_kernel, False, row_taps), row_taps)
    grad_in = chan_sum(adjoint_b, row_halo(adjoint_b), prep_kernel(in_kernel, True, row_taps), row_taps)
    return (mixed, grad_in, grad_decay)


def solution(mesh):
    placed = (
        P(("grp", "tm"), "rows", None, None),
        P(None, None, None, "chan"),
        P(None, None, "chan", None),
        P("chan"),
        P("grp"),
        P(("grp", "tm"), "rows", None, None),
    )
    return jax.shard_map(
        local,
        mesh=mesh,
        in_specs=placed,
        out_specs=(
            P(("grp", "tm"), "rows", None, "chan"),
            P(("grp", "tm"), "rows", None, "chan"),
            P(("grp", "chan")),
        ),
        check_vma=False,
    )
```

```python
import math

import jax
import jax.numpy as jnp
from jax import lax
from jax.sharding import PartitionSpec as P


def row_halo(cells):
    count = lax.axis_size("rows")
    if count == 1:
        return None
    ends = count - 1
    head = cells[:, :1]
    tail = cells[:, -1:]
    top = lax.ppermute(tail, "rows", [(i, i + 1) for i in range(ends)])
    bottom = lax.ppermute(head, "rows", [(i + 1, i) for i in range(ends)])
    return top, bottom


def row_taps_of(halo, row_count):
    return (1,) if halo is None and row_count == 1 else (0, 1, 2)


def prep_kernel(kernel, transpose, row_taps):
    if transpose:
        flipped = kernel[::-1, ::-1]
        taps = jnp.stack([flipped[a] for a in row_taps])
        taps = jnp.swapaxes(taps, 2, 3)
    else:
        taps = jnp.stack([kernel[a] for a in row_taps])
    return lax.optimization_barrier(taps)


def conv_apply(cells, halo, taps, row_taps):
    frame_count, row_count, col_count, channels = cells.shape
    if len(row_taps) == 1:
        extended = jnp.pad(cells, ((0, 0), (1, 1), (0, 0), (0, 0)))
    else:
        if halo is None:
            zero = jnp.zeros_like(cells[:, :1])
            halo = (zero, zero)
        extended = jnp.concatenate([halo[0], cells, halo[1]], axis=1)
    padded = jnp.pad(extended, ((0, 0), (0, 0), (1, 1), (0, 0)))
    summed = None
    for index, row_tap in enumerate(row_taps):
        for col_tap in range(3):
            portion = padded[:, row_tap : row_tap + row_count, col_tap : col_tap + col_count, :]
            term = jnp.dot(
                portion.reshape(-1, channels),
                taps[index, col_tap],
                preferred_element_type=jnp.float32,
            )
            summed = term if summed is None else summed + term
    return summed.reshape(frame_count, row_count, col_count, -1)


def all_sum(value, axis):
    count = lax.axis_size(axis)
    if count == 1:
        return value
    mine = lax.axis_index(axis)
    got = [value] + [
        lax.ppermute(value, axis, [(i, (i + step) % count) for i in range(count)])
        for step in range(1, count)
    ]
    stacked = jnp.stack(got)
    ordered = jnp.take(stacked, (mine - jnp.arange(count)) % count, axis=0)
    total = ordered[0]
    for index in range(1, count):
        total = total + ordered[index]
    return total


def chan_sum(cells, halo, taps, row_taps):
    count = lax.axis_size("chan")
    mine = lax.axis_index("chan")
    width = taps.shape[3] // count
    if count != 2:
        part = conv_apply(cells, halo, taps, row_taps)
        return lax.psum_scatter(part.astype(jnp.bfloat16), "chan", scatter_dimension=3, tiled=True)
    other_taps = lax.dynamic_slice_in_dim(taps, (1 - mine) * width, width, axis=3)
    own_taps = lax.dynamic_slice_in_dim(taps, mine * width, width, axis=3)
    other = conv_apply(cells, halo, other_taps, row_taps).astype(jnp.bfloat16)
    got = lax.ppermute(other, "chan", [(0, 1), (1, 0)])
    own = conv_apply(cells, halo, own_taps, row_taps)
    return (own + got.astype(jnp.float32)).astype(jnp.bfloat16)


def block_carries(fwd_end, bwd_start, fwd_prod, bwd_prod, axis):
    count = lax.axis_size(axis)
    mine = lax.axis_index(axis)
    received = {}
    for step in range(1, count):
        message = jnp.where(mine + step < count, fwd_end, bwd_start)
        received[step] = lax.ppermute(message, axis, [(i, (i + step) % count) for i in range(count)])
    carry_in = jnp.zeros_like(fwd_end)
    for step in reversed(range(1, count)):
        source = mine - step
        factor = lax.dynamic_index_in_dim(fwd_prod, jnp.maximum(source, 0), 0, keepdims=False)
        carry_in = jnp.where(source >= 0, received[step], 0.0) + factor * carry_in
    carry_back = jnp.zeros_like(bwd_start)
    for step in reversed(range(1, count)):
        source = mine + step
        factor = lax.dynamic_index_in_dim(bwd_prod, jnp.minimum(source, count - 1), 0, keepdims=False)
        carry_back = jnp.where(source < count, received[count - step], 0.0) + factor * carry_back
    return carry_in, carry_back


def local(frames_in, in_kernel, out_kernel, decay_rate, frame_keep, out_grad):
    frame_count, row_count, col_count = frames_in.shape[:3]
    position = lax.axis_index("tm")
    blocks = lax.axis_size("tm")
    in_halo = row_halo(frames_in)
    grad_halo = row_halo(out_grad)
    row_taps = row_taps_of(in_halo, row_count)
    values = conv_apply(frames_in, in_halo, prep_kernel(in_kernel, False, row_taps), row_taps)
    adjoint_in = conv_apply(out_grad, grad_halo, prep_kernel(out_kernel, True, row_taps), row_taps)
    input_gain = jnp.sqrt(1.0 - decay_rate * decay_rate)
    keep_padded = jnp.concatenate([frame_keep, jnp.zeros((1,), jnp.float32)])
    offset = position * frame_count
    keep_here = lax.dynamic_slice_in_dim(keep_padded, offset, frame_count)
    keep_next = lax.dynamic_slice_in_dim(keep_padded, offset + 1, frame_count)
    decays = keep_here[:, None] * decay_rate[None, :]
    decays_next = keep_next[:, None] * decay_rate[None, :]

    running = None
    product = None
    local_states, products = [], []
    for t in range(frame_count):
        fresh = input_gain * values[t]
        running = fresh if running is None else decays[t] * running + fresh
        product = decays[t] if product is None else product * decays[t]
        local_states.append(running)
        products.append(product)
    running = None
    product = None
    back_states, back_products = [None] * frame_count, [None] * frame_count
    for t in reversed(range(frame_count)):
        running = adjoint_in[t] if running is None else adjoint_in[t] + decays_next[t] * running
        product = decays_next[t] if product is None else product * decays_next[t]
        back_states[t] = running
        back_products[t] = product

    all_decays = (frame_keep[:, None] * decay_rate[None, :]).reshape(blocks, frame_count, -1)
    all_next = (keep_padded[1:, None] * decay_rate[None, :]).reshape(blocks, frame_count, -1)
    fwd_prod = all_decays[:, 0]
    for t in range(1, frame_count):
        fwd_prod = fwd_prod * all_decays[:, t]
    bwd_prod = all_next[:, frame_count - 1]
    for t in reversed(range(frame_count - 1)):
        bwd_prod = bwd_prod * all_next[:, t]
    carry_in, carry_back = block_carries(local_states[-1], back_states[0], fwd_prod, bwd_prod, "tm")

    states = jnp.stack([local_states[t] + products[t] * carry_in for t in range(frame_count)])
    adjoints = jnp.stack([back_states[t] + back_products[t] * carry_back for t in range(frame_count)])
    previous = jnp.concatenate([carry_in[None], states[:-1]], axis=0)
    terms = adjoints * (
        decays[:, None, None, :] * previous - decay_rate * decay_rate / input_gain * values
    )
    total_count = frame_count * blocks * row_count * lax.axis_size("rows") * col_count
    grad_decay = all_sum(all_sum(jnp.sum(terms, axis=(0, 1, 2)), "tm"), "rows") / math.sqrt(total_count)

    state_b = states.astype(jnp.bfloat16)
    adjoint_b = adjoints.astype(jnp.bfloat16)
    mixed = chan_sum(state_b, row_halo(state_b), prep_kernel(out_kernel, False, row_taps), row_taps)
    grad_in = chan_sum(adjoint_b, row_halo(adjoint_b), prep_kernel(in_kernel, True, row_taps), row_taps)
    return (mixed, grad_in, grad_decay)


def solution(mesh):
    placed = (
        P(("grp", "tm"), "rows", None, None),
        P(None, None, None, "chan"),
        P(None, None, "chan", None),
        P("chan"),
        P("grp"),
        P(("grp", "tm"), "rows", None, None),
    )
    return jax.shard_map(
        local,
        mesh=mesh,
        in_specs=placed,
        out_specs=(
            P(("grp", "tm"), "rows", None, "chan"),
            P(("grp", "tm"), "rows", None, "chan"),
            P(("grp", "chan")),
        ),
        check_vma=False,
    )
```

```python
import math

import jax
import jax.numpy as jnp
from jax import lax
from jax.sharding import PartitionSpec as P


def row_halo(cells):
    count = lax.axis_size("rows")
    if count == 1:
        return None
    ends = count - 1
    head = cells[:, :1]
    tail = cells[:, -1:]
    top = lax.ppermute(tail, "rows", [(i, i + 1) for i in range(ends)])
    bottom = lax.ppermute(head, "rows", [(i + 1, i) for i in range(ends)])
    return top, bottom


def row_taps_of(halo, row_count):
    return (1,) if halo is None and row_count == 1 else (0, 1, 2)


def prep_kernel(kernel, transpose, row_taps):
    if transpose:
        flipped = kernel[::-1, ::-1]
        taps = jnp.stack([flipped[a] for a in row_taps])
        taps = jnp.swapaxes(taps, 2, 3)
    else:
        taps = jnp.stack([kernel[a] for a in row_taps])
    return lax.optimization_barrier(taps)


def conv_apply(cells, halo, taps, row_taps):
    frame_count, row_count, col_count, channels = cells.shape
    if len(row_taps) == 1:
        extended = jnp.pad(cells, ((0, 0), (1, 1), (0, 0), (0, 0)))
    else:
        if halo is None:
            zero = jnp.zeros_like(cells[:, :1])
            halo = (zero, zero)
        extended = jnp.concatenate([halo[0], cells, halo[1]], axis=1)
    padded = jnp.pad(extended, ((0, 0), (0, 0), (1, 1), (0, 0)))
    summed = None
    for index, row_tap in enumerate(row_taps):
        for col_tap in range(3):
            portion = padded[:, row_tap : row_tap + row_count, col_tap : col_tap + col_count, :]
            term = jnp.dot(
                portion.reshape(-1, channels),
                taps[index, col_tap],
                preferred_element_type=jnp.float32,
            )
            summed = term if summed is None else summed + term
    return summed.reshape(frame_count, row_count, col_count, -1)


def all_sum(value, axis):
    count = lax.axis_size(axis)
    if count == 1:
        return value
    if count & (count - 1) == 0:
        step = 1
        while step < count:
            value = value + lax.ppermute(value, axis, [(i, i ^ step) for i in range(count)])
            step *= 2
        return value
    return lax.psum(value, axis)


def chan_sum(cells, halo, taps, row_taps):
    count = lax.axis_size("chan")
    mine = lax.axis_index("chan")
    width = taps.shape[3] // count
    if count != 2:
        part = conv_apply(cells, halo, taps, row_taps)
        return lax.psum_scatter(part.astype(jnp.bfloat16), "chan", scatter_dimension=3, tiled=True)
    other_taps = lax.dynamic_slice_in_dim(taps, (1 - mine) * width, width, axis=3)
    own_taps = lax.dynamic_slice_in_dim(taps, mine * width, width, axis=3)
    other = conv_apply(cells, halo, other_taps, row_taps).astype(jnp.bfloat16)
    got = lax.ppermute(other, "chan", [(0, 1), (1, 0)])
    own = conv_apply(cells, halo, own_taps, row_taps)
    return (own + got.astype(jnp.float32)).astype(jnp.bfloat16)


def block_carries(fwd_end, bwd_start, fwd_prod, bwd_prod, axis):
    count = lax.axis_size(axis)
    mine = lax.axis_index(axis)
    later = (lax.broadcasted_iota(jnp.int32, (count,) + (1,) * fwd_end.ndim, 0) > mine)
    outgoing = jnp.where(later, fwd_end[None], bwd_start[None])
    incoming = lax.all_to_all(outgoing, axis, 0, 0, tiled=True)
    received = {
        step: lax.dynamic_index_in_dim(incoming, (mine - step) % count, 0, keepdims=False)
        for step in range(1, count)
    }
    carry_in = jnp.zeros_like(fwd_end)
    for step in reversed(range(1, count)):
        source = mine - step
        factor = lax.dynamic_index_in_dim(fwd_prod, jnp.maximum(source, 0), 0, keepdims=False)
        carry_in = jnp.where(source >= 0, received[step], 0.0) + factor * carry_in
    carry_back = jnp.zeros_like(bwd_start)
    for step in reversed(range(1, count)):
        source = mine + step
        factor = lax.dynamic_index_in_dim(bwd_prod, jnp.minimum(source, count - 1), 0, keepdims=False)
        carry_back = jnp.where(source < count, received[count - step], 0.0) + factor * carry_back
    return carry_in, carry_back


def local(frames_in, in_kernel, out_kernel, decay_rate, frame_keep, out_grad):
    frame_count, row_count, col_count = frames_in.shape[:3]
    position = lax.axis_index("tm")
    blocks = lax.axis_size("tm")
    in_halo = row_halo(frames_in)
    grad_halo = row_halo(out_grad)
    row_taps = row_taps_of(in_halo, row_count)
    values = conv_apply(frames_in, in_halo, prep_kernel(in_kernel, False, row_taps), row_taps)
    adjoint_in = conv_apply(out_grad, grad_halo, prep_kernel(out_kernel, True, row_taps), row_taps)
    input_gain = jnp.sqrt(1.0 - decay_rate * decay_rate)
    keep_padded = jnp.concatenate([frame_keep, jnp.zeros((1,), jnp.float32)])
    offset = position * frame_count
    keep_here = lax.dynamic_slice_in_dim(keep_padded, offset, frame_count)
    keep_next = lax.dynamic_slice_in_dim(keep_padded, offset + 1, frame_count)
    decays = keep_here[:, None] * decay_rate[None, :]
    decays_next = keep_next[:, None] * decay_rate[None, :]

    running = None
    product = None
    local_states, products = [], []
    for t in range(frame_count):
        fresh = input_gain * values[t]
        running = fresh if running is None else decays[t] * running + fresh
        product = decays[t] if product is None else product * decays[t]
        local_states.append(running)
        products.append(product)
    running = None
    product = None
    back_states, back_products = [None] * frame_count, [None] * frame_count
    for t in reversed(range(frame_count)):
        running = adjoint_in[t] if running is None else adjoint_in[t] + decays_next[t] * running
        product = decays_next[t] if product is None else product * decays_next[t]
        back_states[t] = running
        back_products[t] = product

    all_decays = (frame_keep[:, None] * decay_rate[None, :]).reshape(blocks, frame_count, -1)
    all_next = (keep_padded[1:, None] * decay_rate[None, :]).reshape(blocks, frame_count, -1)
    fwd_prod = all_decays[:, 0]
    for t in range(1, frame_count):
        fwd_prod = fwd_prod * all_decays[:, t]
    bwd_prod = all_next[:, frame_count - 1]
    for t in reversed(range(frame_count - 1)):
        bwd_prod = bwd_prod * all_next[:, t]
    carry_in, carry_back = block_carries(local_states[-1], back_states[0], fwd_prod, bwd_prod, "tm")

    states = jnp.stack([local_states[t] + products[t] * carry_in for t in range(frame_count)])
    adjoints = jnp.stack([back_states[t] + back_products[t] * carry_back for t in range(frame_count)])
    previous = jnp.concatenate([carry_in[None], states[:-1]], axis=0)
    terms = adjoints * (
        decays[:, None, None, :] * previous - decay_rate * decay_rate / input_gain * values
    )
    total_count = frame_count * blocks * row_count * lax.axis_size("rows") * col_count
    grad_decay = all_sum(all_sum(jnp.sum(terms, axis=(0, 1, 2)), "tm"), "rows") / math.sqrt(total_count)

    state_b = states.astype(jnp.bfloat16)
    adjoint_b = adjoints.astype(jnp.bfloat16)
    mixed = chan_sum(state_b, row_halo(state_b), prep_kernel(out_kernel, False, row_taps), row_taps)
    grad_in = chan_sum(adjoint_b, row_halo(adjoint_b), prep_kernel(in_kernel, True, row_taps), row_taps)
    return (mixed, grad_in, grad_decay)


def solution(mesh):
    placed = (
        P(("grp", "tm"), "rows", None, None),
        P(None, None, None, "chan"),
        P(None, None, "chan", None),
        P("chan"),
        P("grp"),
        P(("grp", "tm"), "rows", None, None),
    )
    return jax.shard_map(
        local,
        mesh=mesh,
        in_specs=placed,
        out_specs=(
            P(("grp", "tm"), "rows", None, "chan"),
            P(("grp", "tm"), "rows", None, "chan"),
            P(("grp", "chan")),
        ),
        check_vma=False,
    )
```

```python
import math

import jax
import jax.numpy as jnp
from jax import lax
from jax.sharding import PartitionSpec as P


def row_halo(cells):
    count = lax.axis_size("rows")
    if count == 1:
        return None
    ends = count - 1
    head = cells[:, :1]
    tail = cells[:, -1:]
    top = lax.ppermute(tail, "rows", [(i, i + 1) for i in range(ends)])
    bottom = lax.ppermute(head, "rows", [(i + 1, i) for i in range(ends)])
    return top, bottom


def row_taps_of(halo, row_count):
    return (1,) if halo is None and row_count == 1 else (0, 1, 2)


def prep_kernel(kernel, transpose, row_taps):
    if transpose:
        flipped = kernel[::-1, ::-1]
        taps = jnp.stack([flipped[a] for a in row_taps])
        taps = jnp.swapaxes(taps, 2, 3)
    else:
        taps = jnp.stack([kernel[a] for a in row_taps])
    return lax.optimization_barrier(taps)


def conv_apply(cells, halo, taps, row_taps):
    frame_count, row_count, col_count, channels = cells.shape
    if len(row_taps) == 1:
        extended = jnp.pad(cells, ((0, 0), (1, 1), (0, 0), (0, 0)))
    else:
        if halo is None:
            zero = jnp.zeros_like(cells[:, :1])
            halo = (zero, zero)
        extended = jnp.concatenate([halo[0], cells, halo[1]], axis=1)
    padded = jnp.pad(extended, ((0, 0), (0, 0), (1, 1), (0, 0)))
    summed = None
    for index, row_tap in enumerate(row_taps):
        for col_tap in range(3):
            portion = padded[:, row_tap : row_tap + row_count, col_tap : col_tap + col_count, :]
            term = jnp.dot(
                portion.reshape(-1, channels),
                taps[index, col_tap],
                preferred_element_type=jnp.float32,
            )
            summed = term if summed is None else summed + term
    return summed.reshape(frame_count, row_count, col_count, -1)


def all_sum(value, axis):
    count = lax.axis_size(axis)
    if count == 1:
        return value
    if count & (count - 1) == 0:
        step = 1
        while step < count:
            value = value + lax.ppermute(value, axis, [(i, i ^ step) for i in range(count)])
            step *= 2
        return value
    return lax.psum(value, axis)


def chan_sum(cells, halo, taps, row_taps):
    count = lax.axis_size("chan")
    mine = lax.axis_index("chan")
    width = taps.shape[3] // count
    if count != 2:
        part = conv_apply(cells, halo, taps, row_taps)
        return lax.psum_scatter(part.astype(jnp.bfloat16), "chan", scatter_dimension=3, tiled=True)
    other_taps = lax.dynamic_slice_in_dim(taps, (1 - mine) * width, width, axis=3)
    own_taps = lax.dynamic_slice_in_dim(taps, mine * width, width, axis=3)
    other = conv_apply(cells, halo, other_taps, row_taps).astype(jnp.bfloat16)
    got = lax.ppermute(other, "chan", [(0, 1), (1, 0)])
    own = conv_apply(cells, halo, own_taps, row_taps)
    return (own + got.astype(jnp.float32)).astype(jnp.bfloat16)


def block_carries(fwd_end, bwd_start, fwd_prod, bwd_prod, axis):
    count = lax.axis_size(axis)
    mine = lax.axis_index(axis)
    if count % 2 == 0 and count > 2:
        return paired_carries(fwd_end, bwd_start, fwd_prod, bwd_prod, axis)
    received = {}
    for step in range(1, count):
        message = jnp.where(mine + step < count, fwd_end, bwd_start)
        received[step] = lax.ppermute(message, axis, [(i, (i + step) % count) for i in range(count)])
    carry_in = jnp.zeros_like(fwd_end)
    for step in reversed(range(1, count)):
        source = mine - step
        factor = lax.dynamic_index_in_dim(fwd_prod, jnp.maximum(source, 0), 0, keepdims=False)
        carry_in = jnp.where(source >= 0, received[step], 0.0) + factor * carry_in
    carry_back = jnp.zeros_like(bwd_start)
    for step in reversed(range(1, count)):
        source = mine + step
        factor = lax.dynamic_index_in_dim(bwd_prod, jnp.minimum(source, count - 1), 0, keepdims=False)
        carry_back = jnp.where(source < count, received[count - step], 0.0) + factor * carry_back
    return carry_in, carry_back


def paired_carries(fwd_end, bwd_start, fwd_prod, bwd_prod, axis):
    count = lax.axis_size(axis)
    pairs_count = count // 2
    mine = lax.axis_index(axis)
    upper = mine % 2 == 1
    pair = mine // 2
    swap = [(i, i ^ 1) for i in range(count)]

    def pick(table, index):
        return lax.dynamic_index_in_dim(table, jnp.clip(index, 0, table.shape[0] - 1), 0, keepdims=False)

    partner = lax.ppermute(jnp.where(upper, bwd_start, fwd_end), axis, swap)
    aggregate = jnp.where(
        upper,
        fwd_end + pick(fwd_prod, mine) * partner,
        bwd_start + pick(bwd_prod, mine) * partner,
    )
    pair_fwd = fwd_prod[1::2] * fwd_prod[0::2]
    pair_bwd = bwd_prod[0::2] * bwd_prod[1::2]
    received = {}
    for step in range(1, pairs_count):
        links = [(2 * z + 1, 2 * (z + step) + 1) for z in range(pairs_count - step)]
        links += [(2 * z, 2 * (z - step)) for z in range(step, pairs_count)]
        received[step] = lax.ppermute(aggregate, axis, links)
    outer = jnp.zeros_like(aggregate)
    for step in reversed(range(1, pairs_count)):
        valid = jnp.where(upper, pair - step >= 0, pair + step < pairs_count)
        factor = jnp.where(upper, pick(pair_fwd, pair - step), pick(pair_bwd, pair + step))
        outer = jnp.where(valid, received[step], 0.0) + factor * outer
    other = lax.ppermute(outer, axis, swap)
    carry_in = jnp.where(upper, partner + pick(fwd_prod, mine - 1) * outer, other)
    carry_back = jnp.where(upper, other, partner + pick(bwd_prod, mine + 1) * outer)
    return carry_in, carry_back


def local(frames_in, in_kernel, out_kernel, decay_rate, frame_keep, out_grad):
    frame_count, row_count, col_count = frames_in.shape[:3]
    position = lax.axis_index("tm")
    blocks = lax.axis_size("tm")
    in_halo = row_halo(frames_in)
    grad_halo = row_halo(out_grad)
    row_taps = row_taps_of(in_halo, row_count)
    values = conv_apply(frames_in, in_halo, prep_kernel(in_kernel, False, row_taps), row_taps)
    adjoint_in = conv_apply(out_grad, grad_halo, prep_kernel(out_kernel, True, row_taps), row_taps)
    input_gain = jnp.sqrt(1.0 - decay_rate * decay_rate)
    keep_padded = jnp.concatenate([frame_keep, jnp.zeros((1,), jnp.float32)])
    offset = position * frame_count
    keep_here = lax.dynamic_slice_in_dim(keep_padded, offset, frame_count)
    keep_next = lax.dynamic_slice_in_dim(keep_padded, offset + 1, frame_count)
    decays = keep_here[:, None] * decay_rate[None, :]
    decays_next = keep_next[:, None] * decay_rate[None, :]

    running = None
    product = None
    local_states, products = [], []
    for t in range(frame_count):
        fresh = input_gain * values[t]
        running = fresh if running is None else decays[t] * running + fresh
        product = decays[t] if product is None else product * decays[t]
        local_states.append(running)
        products.append(product)
    running = None
    product = None
    back_states, back_products = [None] * frame_count, [None] * frame_count
    for t in reversed(range(frame_count)):
        running = adjoint_in[t] if running is None else adjoint_in[t] + decays_next[t] * running
        product = decays_next[t] if product is None else product * decays_next[t]
        back_states[t] = running
        back_products[t] = product

    all_decays = (frame_keep[:, None] * decay_rate[None, :]).reshape(blocks, frame_count, -1)
    all_next = (keep_padded[1:, None] * decay_rate[None, :]).reshape(blocks, frame_count, -1)
    fwd_prod = all_decays[:, 0]
    for t in range(1, frame_count):
        fwd_prod = fwd_prod * all_decays[:, t]
    bwd_prod = all_next[:, frame_count - 1]
    for t in reversed(range(frame_count - 1)):
        bwd_prod = bwd_prod * all_next[:, t]
    carry_in, carry_back = block_carries(local_states[-1], back_states[0], fwd_prod, bwd_prod, "tm")

    states = jnp.stack([local_states[t] + products[t] * carry_in for t in range(frame_count)])
    adjoints = jnp.stack([back_states[t] + back_products[t] * carry_back for t in range(frame_count)])
    previous = jnp.concatenate([carry_in[None], states[:-1]], axis=0)
    terms = adjoints * (
        decays[:, None, None, :] * previous - decay_rate * decay_rate / input_gain * values
    )
    total_count = frame_count * blocks * row_count * lax.axis_size("rows") * col_count
    grad_decay = all_sum(all_sum(jnp.sum(terms, axis=(0, 1, 2)), "tm"), "rows") / math.sqrt(total_count)

    state_b = states.astype(jnp.bfloat16)
    adjoint_b = adjoints.astype(jnp.bfloat16)
    mixed = chan_sum(state_b, row_halo(state_b), prep_kernel(out_kernel, False, row_taps), row_taps)
    grad_in = chan_sum(adjoint_b, row_halo(adjoint_b), prep_kernel(in_kernel, True, row_taps), row_taps)
    return (mixed, grad_in, grad_decay)


def solution(mesh):
    placed = (
        P(("grp", "tm"), "rows", None, None),
        P(None, None, None, "chan"),
        P(None, None, "chan", None),
        P("chan"),
        P("grp"),
        P(("grp", "tm"), "rows", None, None),
    )
    return jax.shard_map(
        local,
        mesh=mesh,
        in_specs=placed,
        out_specs=(
            P(("grp", "tm"), "rows", None, "chan"),
            P(("grp", "tm"), "rows", None, "chan"),
            P(("grp", "chan")),
        ),
        check_vma=False,
    )
```

```python
import math

import jax
import jax.numpy as jnp
from jax import lax
from jax.sharding import PartitionSpec as P


def row_halo(cells):
    count = lax.axis_size("rows")
    if count == 1:
        return None
    ends = count - 1
    head = cells[:, :1]
    tail = cells[:, -1:]
    top = lax.ppermute(tail, "rows", [(i, i + 1) for i in range(ends)])
    bottom = lax.ppermute(head, "rows", [(i + 1, i) for i in range(ends)])
    return top, bottom


def row_taps_of(halo, row_count):
    return (1,) if halo is None and row_count == 1 else (0, 1, 2)


def prep_kernel(kernel, transpose, row_taps):
    if transpose:
        flipped = kernel[::-1, ::-1]
        taps = jnp.stack([flipped[a] for a in row_taps])
        taps = jnp.swapaxes(taps, 2, 3)
    else:
        taps = jnp.stack([kernel[a] for a in row_taps])
    return lax.optimization_barrier(taps)


def conv_apply(cells, halo, taps, row_taps):
    frame_count, row_count, col_count, channels = cells.shape
    if len(row_taps) == 1:
        extended = jnp.pad(cells, ((0, 0), (1, 1), (0, 0), (0, 0)))
    else:
        if halo is None:
            zero = jnp.zeros_like(cells[:, :1])
            halo = (zero, zero)
        extended = jnp.concatenate([halo[0], cells, halo[1]], axis=1)
    padded = jnp.pad(extended, ((0, 0), (0, 0), (1, 1), (0, 0)))
    summed = None
    for index, row_tap in enumerate(row_taps):
        for col_tap in range(3):
            portion = padded[:, row_tap : row_tap + row_count, col_tap : col_tap + col_count, :]
            term = jnp.dot(
                portion.reshape(-1, channels),
                taps[index, col_tap],
                preferred_element_type=jnp.float32,
            )
            summed = term if summed is None else summed + term
    return summed.reshape(frame_count, row_count, col_count, -1)


def all_sum(value, axis):
    count = lax.axis_size(axis)
    if count == 1:
        return value
    outgoing = jnp.broadcast_to(value[None], (count,) + value.shape)
    incoming = lax.all_to_all(outgoing, axis, 0, 0, tiled=True)
    total = incoming[0]
    for index in range(1, count):
        total = total + incoming[index]
    return total


def chan_sum(cells, halo, taps, row_taps):
    count = lax.axis_size("chan")
    mine = lax.axis_index("chan")
    width = taps.shape[3] // count
    if count != 2:
        part = conv_apply(cells, halo, taps, row_taps)
        return lax.psum_scatter(part.astype(jnp.bfloat16), "chan", scatter_dimension=3, tiled=True)
    other_taps = lax.dynamic_slice_in_dim(taps, (1 - mine) * width, width, axis=3)
    own_taps = lax.dynamic_slice_in_dim(taps, mine * width, width, axis=3)
    other = conv_apply(cells, halo, other_taps, row_taps).astype(jnp.bfloat16)
    got = lax.ppermute(other, "chan", [(0, 1), (1, 0)])
    own = conv_apply(cells, halo, own_taps, row_taps)
    return (own + got.astype(jnp.float32)).astype(jnp.bfloat16)


def block_carries(fwd_end, bwd_start, fwd_prod, bwd_prod, axis):
    count = lax.axis_size(axis)
    mine = lax.axis_index(axis)
    if count % 2 == 0 and count > 2:
        return paired_carries(fwd_end, bwd_start, fwd_prod, bwd_prod, axis)
    received = {}
    for step in range(1, count):
        message = jnp.where(mine + step < count, fwd_end, bwd_start)
        received[step] = lax.ppermute(message, axis, [(i, (i + step) % count) for i in range(count)])
    carry_in = jnp.zeros_like(fwd_end)
    for step in reversed(range(1, count)):
        source = mine - step
        factor = lax.dynamic_index_in_dim(fwd_prod, jnp.maximum(source, 0), 0, keepdims=False)
        carry_in = jnp.where(source >= 0, received[step], 0.0) + factor * carry_in
    carry_back = jnp.zeros_like(bwd_start)
    for step in reversed(range(1, count)):
        source = mine + step
        factor = lax.dynamic_index_in_dim(bwd_prod, jnp.minimum(source, count - 1), 0, keepdims=False)
        carry_back = jnp.where(source < count, received[count - step], 0.0) + factor * carry_back
    return carry_in, carry_back


def paired_carries(fwd_end, bwd_start, fwd_prod, bwd_prod, axis):
    count = lax.axis_size(axis)
    pairs_count = count // 2
    mine = lax.axis_index(axis)
    upper = mine % 2 == 1
    pair = mine // 2
    swap = [(i, i ^ 1) for i in range(count)]

    def pick(table, index):
        return lax.dynamic_index_in_dim(table, jnp.clip(index, 0, table.shape[0] - 1), 0, keepdims=False)

    partner = lax.ppermute(jnp.where(upper, bwd_start, fwd_end), axis, swap)
    aggregate = jnp.where(
        upper,
        fwd_end + pick(fwd_prod, mine) * partner,
        bwd_start + pick(bwd_prod, mine) * partner,
    )
    pair_fwd = fwd_prod[1::2] * fwd_prod[0::2]
    pair_bwd = bwd_prod[0::2] * bwd_prod[1::2]
    received = {}
    for step in range(1, pairs_count):
        links = [(2 * z + 1, 2 * (z + step) + 1) for z in range(pairs_count - step)]
        links += [(2 * z, 2 * (z - step)) for z in range(step, pairs_count)]
        received[step] = lax.ppermute(aggregate, axis, links)
    outer = jnp.zeros_like(aggregate)
    for step in reversed(range(1, pairs_count)):
        valid = jnp.where(upper, pair - step >= 0, pair + step < pairs_count)
        factor = jnp.where(upper, pick(pair_fwd, pair - step), pick(pair_bwd, pair + step))
        outer = jnp.where(valid, received[step], 0.0) + factor * outer
    other = lax.ppermute(outer, axis, swap)
    carry_in = jnp.where(upper, partner + pick(fwd_prod, mine - 1) * outer, other)
    carry_back = jnp.where(upper, other, partner + pick(bwd_prod, mine + 1) * outer)
    return carry_in, carry_back


def local(frames_in, in_kernel, out_kernel, decay_rate, frame_keep, out_grad):
    frame_count, row_count, col_count = frames_in.shape[:3]
    position = lax.axis_index("tm")
    blocks = lax.axis_size("tm")
    in_halo = row_halo(frames_in)
    grad_halo = row_halo(out_grad)
    row_taps = row_taps_of(in_halo, row_count)
    values = conv_apply(frames_in, in_halo, prep_kernel(in_kernel, False, row_taps), row_taps)
    adjoint_in = conv_apply(out_grad, grad_halo, prep_kernel(out_kernel, True, row_taps), row_taps)
    input_gain = jnp.sqrt(1.0 - decay_rate * decay_rate)
    keep_padded = jnp.concatenate([frame_keep, jnp.zeros((1,), jnp.float32)])
    offset = position * frame_count
    keep_here = lax.dynamic_slice_in_dim(keep_padded, offset, frame_count)
    keep_next = lax.dynamic_slice_in_dim(keep_padded, offset + 1, frame_count)
    decays = keep_here[:, None] * decay_rate[None, :]
    decays_next = keep_next[:, None] * decay_rate[None, :]

    running = None
    product = None
    local_states, products = [], []
    for t in range(frame_count):
        fresh = input_gain * values[t]
        running = fresh if running is None else decays[t] * running + fresh
        product = decays[t] if product is None else product * decays[t]
        local_states.append(running)
        products.append(product)
    running = None
    product = None
    back_states, back_products = [None] * frame_count, [None] * frame_count
    for t in reversed(range(frame_count)):
        running = adjoint_in[t] if running is None else adjoint_in[t] + decays_next[t] * running
        product = decays_next[t] if product is None else product * decays_next[t]
        back_states[t] = running
        back_products[t] = product

    all_decays = (frame_keep[:, None] * decay_rate[None, :]).reshape(blocks, frame_count, -1)
    all_next = (keep_padded[1:, None] * decay_rate[None, :]).reshape(blocks, frame_count, -1)
    fwd_prod = all_decays[:, 0]
    for t in range(1, frame_count):
        fwd_prod = fwd_prod * all_decays[:, t]
    bwd_prod = all_next[:, frame_count - 1]
    for t in reversed(range(frame_count - 1)):
        bwd_prod = bwd_prod * all_next[:, t]
    carry_in, carry_back = block_carries(local_states[-1], back_states[0], fwd_prod, bwd_prod, "tm")

    states = jnp.stack([local_states[t] + products[t] * carry_in for t in range(frame_count)])
    adjoints = jnp.stack([back_states[t] + back_products[t] * carry_back for t in range(frame_count)])
    previous = jnp.concatenate([carry_in[None], states[:-1]], axis=0)
    terms = adjoints * (
        decays[:, None, None, :] * previous - decay_rate * decay_rate / input_gain * values
    )
    total_count = frame_count * blocks * row_count * lax.axis_size("rows") * col_count
    grad_decay = all_sum(all_sum(jnp.sum(terms, axis=(0, 1, 2)), "tm"), "rows") / math.sqrt(total_count)

    state_b = states.astype(jnp.bfloat16)
    adjoint_b = adjoints.astype(jnp.bfloat16)
    mixed = chan_sum(state_b, row_halo(state_b), prep_kernel(out_kernel, False, row_taps), row_taps)
    grad_in = chan_sum(adjoint_b, row_halo(adjoint_b), prep_kernel(in_kernel, True, row_taps), row_taps)
    return (mixed, grad_in, grad_decay)


def solution(mesh):
    placed = (
        P(("grp", "tm"), "rows", None, None),
        P(None, None, None, "chan"),
        P(None, None, "chan", None),
        P("chan"),
        P("grp"),
        P(("grp", "tm"), "rows", None, None),
    )
    return jax.shard_map(
        local,
        mesh=mesh,
        in_specs=placed,
        out_specs=(
            P(("grp", "tm"), "rows", None, "chan"),
            P(("grp", "tm"), "rows", None, "chan"),
            P(("grp", "chan")),
        ),
        check_vma=False,
    )
```

```python
import math

import jax
import jax.numpy as jnp
from jax import lax
from jax.sharding import PartitionSpec as P


def row_halo(cells):
    count = lax.axis_size("rows")
    if count == 1:
        return None
    ends = count - 1
    head = cells[:, :1]
    tail = cells[:, -1:]
    top = lax.ppermute(tail, "rows", [(i, i + 1) for i in range(ends)])
    bottom = lax.ppermute(head, "rows", [(i + 1, i) for i in range(ends)])
    return top, bottom


def row_taps_of(halo, row_count):
    return (1,) if halo is None and row_count == 1 else (0, 1, 2)


def prep_kernel(kernel, transpose, row_taps):
    if transpose:
        flipped = kernel[::-1, ::-1]
        taps = jnp.stack([flipped[a] for a in row_taps])
        taps = jnp.swapaxes(taps, 2, 3)
    else:
        taps = jnp.stack([kernel[a] for a in row_taps])
    return lax.optimization_barrier(taps)


def conv_apply(cells, halo, taps, row_taps):
    frame_count, row_count, col_count, channels = cells.shape
    if len(row_taps) == 1:
        extended = jnp.pad(cells, ((0, 0), (1, 1), (0, 0), (0, 0)))
    else:
        if halo is None:
            zero = jnp.zeros_like(cells[:, :1])
            halo = (zero, zero)
        extended = jnp.concatenate([halo[0], cells, halo[1]], axis=1)
    padded = jnp.pad(extended, ((0, 0), (0, 0), (1, 1), (0, 0)))
    summed = None
    for index, row_tap in enumerate(row_taps):
        for col_tap in range(3):
            portion = padded[:, row_tap : row_tap + row_count, col_tap : col_tap + col_count, :]
            term = jnp.dot(
                portion.reshape(-1, channels),
                taps[index, col_tap],
                preferred_element_type=jnp.float32,
            )
            summed = term if summed is None else summed + term
    return summed.reshape(frame_count, row_count, col_count, -1)


def all_sum(value, axis):
    count = lax.axis_size(axis)
    if count == 1:
        return value
    if count & (count - 1) == 0:
        step = 1
        while step < count:
            value = value + lax.ppermute(value, axis, [(i, i ^ step) for i in range(count)])
            step *= 2
        return value
    return lax.psum(value, axis)


def chan_sum(cells, halo, taps, row_taps):
    count = lax.axis_size("chan")
    mine = lax.axis_index("chan")
    width = taps.shape[3] // count
    if count != 2:
        part = conv_apply(cells, halo, taps, row_taps)
        return lax.psum_scatter(part.astype(jnp.bfloat16), "chan", scatter_dimension=3, tiled=True)
    other_taps = lax.dynamic_slice_in_dim(taps, (1 - mine) * width, width, axis=3)
    own_taps = lax.dynamic_slice_in_dim(taps, mine * width, width, axis=3)
    other = conv_apply(cells, halo, other_taps, row_taps).astype(jnp.bfloat16)
    got = lax.ppermute(other, "chan", [(0, 1), (1, 0)])
    own = conv_apply(cells, halo, own_taps, row_taps)
    return (own + got.astype(jnp.float32)).astype(jnp.bfloat16)


def cyclic_carries(fwd_end, bwd_start, fwd_prod, bwd_prod, axis, index, count, route):
    received = {}
    for step in range(1, count):
        message = jnp.where(index + step < count, fwd_end, bwd_start)
        received[step] = lax.ppermute(message, axis, route(step))
    carry_in = jnp.zeros_like(fwd_end)
    for step in reversed(range(1, count)):
        source = index - step
        factor = lax.dynamic_index_in_dim(fwd_prod, jnp.maximum(source, 0), 0, keepdims=False)
        carry_in = jnp.where(source >= 0, received[step], 0.0) + factor * carry_in
    carry_back = jnp.zeros_like(bwd_start)
    for step in reversed(range(1, count)):
        source = index + step
        factor = lax.dynamic_index_in_dim(bwd_prod, jnp.minimum(source, count - 1), 0, keepdims=False)
        carry_back = jnp.where(source < count, received[count - step], 0.0) + factor * carry_back
    return carry_in, carry_back


def group_sum(value, axis, index, count, route):
    if count == 1:
        return value
    if count & (count - 1):
        return None
    step = 1
    while step < count:
        value = value + lax.ppermute(value, axis, route(step))
        step *= 2
    return value


def local(frames_in, in_kernel, out_kernel, decay_rate, frame_keep, out_grad):
    frame_count, row_count, col_count = frames_in.shape[:3]
    position = lax.axis_index("tm")
    blocks = lax.axis_size("tm")
    width = 2 if blocks % 2 == 0 else 1
    groups = blocks // width
    group = position // width
    upper = position % width == 1
    if width == 2:
        swap = [(i, i ^ 1) for i in range(blocks)]
        other_frames = lax.ppermute(frames_in, "tm", swap)
        other_grad = lax.ppermute(out_grad, "tm", swap)
        frames_in = jnp.where(
            upper,
            jnp.concatenate([other_frames, frames_in]),
            jnp.concatenate([frames_in, other_frames]),
        )
        out_grad = jnp.where(
            upper,
            jnp.concatenate([other_grad, out_grad]),
            jnp.concatenate([out_grad, other_grad]),
        )
    span = frame_count * width
    in_halo = row_halo(frames_in)
    grad_halo = row_halo(out_grad)
    row_taps = row_taps_of(in_halo, row_count)
    values = conv_apply(frames_in, in_halo, prep_kernel(in_kernel, False, row_taps), row_taps)
    adjoint_in = conv_apply(out_grad, grad_halo, prep_kernel(out_kernel, True, row_taps), row_taps)
    input_gain = jnp.sqrt(1.0 - decay_rate * decay_rate)
    keep_padded = jnp.concatenate([frame_keep, jnp.zeros((1,), jnp.float32)])
    offset = group * span
    keep_here = lax.dynamic_slice_in_dim(keep_padded, offset, span)
    keep_next = lax.dynamic_slice_in_dim(keep_padded, offset + 1, span)
    decays = keep_here[:, None] * decay_rate[None, :]
    decays_next = keep_next[:, None] * decay_rate[None, :]

    running = None
    product = None
    local_states, products = [], []
    for t in range(span):
        fresh = input_gain * values[t]
        running = fresh if running is None else decays[t] * running + fresh
        product = decays[t] if product is None else product * decays[t]
        local_states.append(running)
        products.append(product)
    running = None
    product = None
    back_states, back_products = [None] * span, [None] * span
    for t in reversed(range(span)):
        running = adjoint_in[t] if running is None else adjoint_in[t] + decays_next[t] * running
        product = decays_next[t] if product is None else product * decays_next[t]
        back_states[t] = running
        back_products[t] = product

    all_decays = (frame_keep[:, None] * decay_rate[None, :]).reshape(groups, span, -1)
    all_next = (keep_padded[1:, None] * decay_rate[None, :]).reshape(groups, span, -1)
    fwd_prod = all_decays[:, 0]
    for t in range(1, span):
        fwd_prod = fwd_prod * all_decays[:, t]
    bwd_prod = all_next[:, span - 1]
    for t in reversed(range(span - 1)):
        bwd_prod = bwd_prod * all_next[:, t]

    def route(step, cyclic=True):
        return [
            (width * z + x, width * ((z + step) % groups if cyclic else z ^ step) + x)
            for z in range(groups)
            for x in range(width)
        ]

    carry_in, carry_back = cyclic_carries(
        local_states[-1], back_states[0], fwd_prod, bwd_prod, "tm", group, groups, route
    )

    states = jnp.stack([local_states[t] + products[t] * carry_in for t in range(span)])
    adjoints = jnp.stack([back_states[t] + back_products[t] * carry_back for t in range(span)])
    previous = jnp.concatenate([carry_in[None], states[:-1]], axis=0)
    terms = adjoints * (
        decays[:, None, None, :] * previous - decay_rate * decay_rate / input_gain * values
    )
    total_count = frame_count * blocks * row_count * lax.axis_size("rows") * col_count
    partial = jnp.sum(terms, axis=(0, 1, 2))
    summed = group_sum(partial, "tm", group, groups, lambda step: route(step, False))
    if summed is None:
        summed = lax.psum(partial, "tm") / width
    grad_decay = all_sum(summed, "rows") / math.sqrt(total_count)

    if width == 2:
        states = jnp.where(upper, states[frame_count:], states[:frame_count])
        adjoints = jnp.where(upper, adjoints[frame_count:], adjoints[:frame_count])
    state_b = states.astype(jnp.bfloat16)
    adjoint_b = adjoints.astype(jnp.bfloat16)
    mixed = chan_sum(state_b, row_halo(state_b), prep_kernel(out_kernel, False, row_taps), row_taps)
    grad_in = chan_sum(adjoint_b, row_halo(adjoint_b), prep_kernel(in_kernel, True, row_taps), row_taps)
    return (mixed, grad_in, grad_decay)


def solution(mesh):
    placed = (
        P(("grp", "tm"), "rows", None, None),
        P(None, None, None, "chan"),
        P(None, None, "chan", None),
        P("chan"),
        P("grp"),
        P(("grp", "tm"), "rows", None, None),
    )
    return jax.shard_map(
        local,
        mesh=mesh,
        in_specs=placed,
        out_specs=(
            P(("grp", "tm"), "rows", None, "chan"),
            P(("grp", "tm"), "rows", None, "chan"),
            P(("grp", "chan")),
        ),
        check_vma=False,
    )
```

```python
import math

import jax
import jax.numpy as jnp
from jax import lax
from jax.sharding import PartitionSpec as P


def row_halo(cells):
    count = lax.axis_size("rows")
    if count == 1:
        return None
    ends = count - 1
    head = cells[:, :1]
    tail = cells[:, -1:]
    top = lax.ppermute(tail, "rows", [(i, i + 1) for i in range(ends)])
    bottom = lax.ppermute(head, "rows", [(i + 1, i) for i in range(ends)])
    return top, bottom


def row_taps_of(halo, row_count):
    return (1,) if halo is None and row_count == 1 else (0, 1, 2)


def prep_kernel(kernel, transpose, row_taps):
    if transpose:
        flipped = kernel[::-1, ::-1]
        taps = jnp.stack([flipped[a] for a in row_taps])
        taps = jnp.swapaxes(taps, 2, 3)
    else:
        taps = jnp.stack([kernel[a] for a in row_taps])
    return lax.optimization_barrier(taps)


def conv_apply(cells, halo, taps, row_taps):
    frame_count, row_count, col_count, channels = cells.shape
    if len(row_taps) == 1:
        extended = jnp.pad(cells, ((0, 0), (1, 1), (0, 0), (0, 0)))
    else:
        if halo is None:
            zero = jnp.zeros_like(cells[:, :1])
            halo = (zero, zero)
        extended = jnp.concatenate([halo[0], cells, halo[1]], axis=1)
    padded = jnp.pad(extended, ((0, 0), (0, 0), (1, 1), (0, 0)))
    summed = None
    for index, row_tap in enumerate(row_taps):
        for col_tap in range(3):
            portion = padded[:, row_tap : row_tap + row_count, col_tap : col_tap + col_count, :]
            term = jnp.dot(
                portion.reshape(-1, channels),
                taps[index, col_tap],
                preferred_element_type=jnp.float32,
            )
            summed = term if summed is None else summed + term
    return summed.reshape(frame_count, row_count, col_count, -1)


def all_sum(value, axis):
    count = lax.axis_size(axis)
    if count == 1:
        return value
    if count & (count - 1) == 0:
        step = 1
        while step < count:
            value = value + lax.ppermute(value, axis, [(i, i ^ step) for i in range(count)])
            step *= 2
        return value
    return lax.psum(value, axis)


def chan_sum(cells, halo, taps, row_taps):
    count = lax.axis_size("chan")
    mine = lax.axis_index("chan")
    width = taps.shape[3] // count
    if count != 2:
        part = conv_apply(cells, halo, taps, row_taps)
        return lax.psum_scatter(part.astype(jnp.bfloat16), "chan", scatter_dimension=3, tiled=True)
    other_taps = lax.dynamic_slice_in_dim(taps, (1 - mine) * width, width, axis=3)
    own_taps = lax.dynamic_slice_in_dim(taps, mine * width, width, axis=3)
    other = conv_apply(cells, halo, other_taps, row_taps).astype(jnp.bfloat16)
    got = lax.ppermute(other, "chan", [(0, 1), (1, 0)])
    own = conv_apply(cells, halo, own_taps, row_taps)
    return (own + got.astype(jnp.float32)).astype(jnp.bfloat16)


def cyclic_carries(fwd_end, bwd_start, fwd_prod, bwd_prod, axis, index, count, route):
    received = {}
    for step in range(1, count):
        message = jnp.where(index + step < count, fwd_end, bwd_start)
        received[step] = lax.ppermute(message, axis, route(step))
    carry_in = jnp.zeros_like(fwd_end)
    for step in reversed(range(1, count)):
        source = index - step
        factor = lax.dynamic_index_in_dim(fwd_prod, jnp.maximum(source, 0), 0, keepdims=False)
        carry_in = jnp.where(source >= 0, received[step], 0.0) + factor * carry_in
    carry_back = jnp.zeros_like(bwd_start)
    for step in reversed(range(1, count)):
        source = index + step
        factor = lax.dynamic_index_in_dim(bwd_prod, jnp.minimum(source, count - 1), 0, keepdims=False)
        carry_back = jnp.where(source < count, received[count - step], 0.0) + factor * carry_back
    return carry_in, carry_back


def group_sum(value, axis, index, count, route):
    if count == 1:
        return value
    if count & (count - 1):
        return None
    step = 1
    while step < count:
        value = value + lax.ppermute(value, axis, route(step))
        step *= 2
    return value


def local(frames_in, in_kernel, out_kernel, decay_rate, frame_keep, out_grad):
    frame_count, row_count, col_count = frames_in.shape[:3]
    position = lax.axis_index("tm")
    blocks = lax.axis_size("tm")
    width = 2 if blocks % 2 == 0 else 1
    groups = blocks // width
    group = position // width
    upper = position % width == 1
    if width == 2:
        swap = [(i, i ^ 1) for i in range(blocks)]
        if lax.axis_size("chan") == 2:
            first = lax.axis_index("chan") == 0
            got = lax.ppermute(jnp.where(first, frames_in, out_grad), "tm", swap)
            traded = lax.ppermute(got, "chan", [(0, 1), (1, 0)])
            other_frames = jnp.where(first, got, traded)
            other_grad = jnp.where(first, traded, got)
        else:
            other_frames = lax.ppermute(frames_in, "tm", swap)
            other_grad = lax.ppermute(out_grad, "tm", swap)
        frames_in = jnp.where(
            upper,
            jnp.concatenate([other_frames, frames_in]),
            jnp.concatenate([frames_in, other_frames]),
        )
        out_grad = jnp.where(
            upper,
            jnp.concatenate([other_grad, out_grad]),
            jnp.concatenate([out_grad, other_grad]),
        )
    span = frame_count * width
    in_halo = row_halo(frames_in)
    grad_halo = row_halo(out_grad)
    row_taps = row_taps_of(in_halo, row_count)
    values = conv_apply(frames_in, in_halo, prep_kernel(in_kernel, False, row_taps), row_taps)
    adjoint_in = conv_apply(out_grad, grad_halo, prep_kernel(out_kernel, True, row_taps), row_taps)
    input_gain = jnp.sqrt(1.0 - decay_rate * decay_rate)
    keep_padded = jnp.concatenate([frame_keep, jnp.zeros((1,), jnp.float32)])
    offset = group * span
    keep_here = lax.dynamic_slice_in_dim(keep_padded, offset, span)
    keep_next = lax.dynamic_slice_in_dim(keep_padded, offset + 1, span)
    decays = keep_here[:, None] * decay_rate[None, :]
    decays_next = keep_next[:, None] * decay_rate[None, :]

    running = None
    product = None
    local_states, products = [], []
    for t in range(span):
        fresh = input_gain * values[t]
        running = fresh if running is None else decays[t] * running + fresh
        product = decays[t] if product is None else product * decays[t]
        local_states.append(running)
        products.append(product)
    running = None
    product = None
    back_states, back_products = [None] * span, [None] * span
    for t in reversed(range(span)):
        running = adjoint_in[t] if running is None else adjoint_in[t] + decays_next[t] * running
        product = decays_next[t] if product is None else product * decays_next[t]
        back_states[t] = running
        back_products[t] = product

    all_decays = (frame_keep[:, None] * decay_rate[None, :]).reshape(groups, span, -1)
    all_next = (keep_padded[1:, None] * decay_rate[None, :]).reshape(groups, span, -1)
    fwd_prod = all_decays[:, 0]
    for t in range(1, span):
        fwd_prod = fwd_prod * all_decays[:, t]
    bwd_prod = all_next[:, span - 1]
    for t in reversed(range(span - 1)):
        bwd_prod = bwd_prod * all_next[:, t]

    def route(step, cyclic=True):
        return [
            (width * z + x, width * ((z + step) % groups if cyclic else z ^ step) + x)
            for z in range(groups)
            for x in range(width)
        ]

    carry_in, carry_back = cyclic_carries(
        local_states[-1], back_states[0], fwd_prod, bwd_prod, "tm", group, groups, route
    )

    states = jnp.stack([local_states[t] + products[t] * carry_in for t in range(span)])
    adjoints = jnp.stack([back_states[t] + back_products[t] * carry_back for t in range(span)])
    previous = jnp.concatenate([carry_in[None], states[:-1]], axis=0)
    terms = adjoints * (
        decays[:, None, None, :] * previous - decay_rate * decay_rate / input_gain * values
    )
    total_count = frame_count * blocks * row_count * lax.axis_size("rows") * col_count
    partial = jnp.sum(terms, axis=(0, 1, 2))
    summed = group_sum(partial, "tm", group, groups, lambda step: route(step, False))
    if summed is None:
        summed = lax.psum(partial, "tm") / width
    grad_decay = all_sum(summed, "rows") / math.sqrt(total_count)

    if width == 2:
        states = jnp.where(upper, states[frame_count:], states[:frame_count])
        adjoints = jnp.where(upper, adjoints[frame_count:], adjoints[:frame_count])
    state_b = states.astype(jnp.bfloat16)
    adjoint_b = adjoints.astype(jnp.bfloat16)
    mixed = chan_sum(state_b, row_halo(state_b), prep_kernel(out_kernel, False, row_taps), row_taps)
    grad_in = chan_sum(adjoint_b, row_halo(adjoint_b), prep_kernel(in_kernel, True, row_taps), row_taps)
    return (mixed, grad_in, grad_decay)


def solution(mesh):
    placed = (
        P(("grp", "tm"), "rows", None, None),
        P(None, None, None, "chan"),
        P(None, None, "chan", None),
        P("chan"),
        P("grp"),
        P(("grp", "tm"), "rows", None, None),
    )
    return jax.shard_map(
        local,
        mesh=mesh,
        in_specs=placed,
        out_specs=(
            P(("grp", "tm"), "rows", None, "chan"),
            P(("grp", "tm"), "rows", None, "chan"),
            P(("grp", "chan")),
        ),
        check_vma=False,
    )
```

```python
import math

import jax
import jax.numpy as jnp
from jax import lax
from jax.sharding import PartitionSpec as P


def row_halo(cells):
    count = lax.axis_size("rows")
    if count == 1:
        return None
    ends = count - 1
    head = cells[:, :1]
    tail = cells[:, -1:]
    top = lax.ppermute(tail, "rows", [(i, i + 1) for i in range(ends)])
    bottom = lax.ppermute(head, "rows", [(i + 1, i) for i in range(ends)])
    return top, bottom


def row_taps_of(halo, row_count):
    return (1,) if halo is None and row_count == 1 else (0, 1, 2)


def prep_kernel(kernel, transpose, row_taps):
    if transpose:
        flipped = kernel[::-1, ::-1]
        taps = jnp.stack([flipped[a] for a in row_taps])
        taps = jnp.swapaxes(taps, 2, 3)
    else:
        taps = jnp.stack([kernel[a] for a in row_taps])
    return lax.optimization_barrier(taps)


def conv_apply(cells, halo, taps, row_taps):
    frame_count, row_count, col_count, channels = cells.shape
    if len(row_taps) == 1:
        extended = jnp.pad(cells, ((0, 0), (1, 1), (0, 0), (0, 0)))
    else:
        if halo is None:
            zero = jnp.zeros_like(cells[:, :1])
            halo = (zero, zero)
        extended = jnp.concatenate([halo[0], cells, halo[1]], axis=1)
    padded = jnp.pad(extended, ((0, 0), (0, 0), (1, 1), (0, 0)))
    summed = None
    for index, row_tap in enumerate(row_taps):
        for col_tap in range(3):
            portion = padded[:, row_tap : row_tap + row_count, col_tap : col_tap + col_count, :]
            term = jnp.dot(
                portion.reshape(-1, channels),
                taps[index, col_tap],
                preferred_element_type=jnp.float32,
            )
            summed = term if summed is None else summed + term
    return summed.reshape(frame_count, row_count, col_count, -1)


def all_sum(value, axis):
    count = lax.axis_size(axis)
    if count == 1:
        return value
    if count & (count - 1) == 0:
        step = 1
        while step < count:
            value = value + lax.ppermute(value, axis, [(i, i ^ step) for i in range(count)])
            step *= 2
        return value
    return lax.psum(value, axis)


def chan_sum(cells, halo, taps, row_taps):
    count = lax.axis_size("chan")
    mine = lax.axis_index("chan")
    width = taps.shape[3] // count
    if count != 2:
        part = conv_apply(cells, halo, taps, row_taps)
        return lax.psum_scatter(part.astype(jnp.bfloat16), "chan", scatter_dimension=3, tiled=True)
    other_taps = lax.dynamic_slice_in_dim(taps, (1 - mine) * width, width, axis=3)
    own_taps = lax.dynamic_slice_in_dim(taps, mine * width, width, axis=3)
    other = conv_apply(cells, halo, other_taps, row_taps).astype(jnp.bfloat16)
    got = lax.ppermute(other, "chan", [(0, 1), (1, 0)])
    own = conv_apply(cells, halo, own_taps, row_taps)
    return (own + got.astype(jnp.float32)).astype(jnp.bfloat16)


def cyclic_carries(fwd_end, bwd_start, fwd_prod, bwd_prod, axis, index, count, route):
    received = {}
    for step in range(1, count):
        message = jnp.where(index + step < count, fwd_end, bwd_start)
        received[step] = lax.ppermute(message, axis, route(step))
    carry_in = jnp.zeros_like(fwd_end)
    for step in reversed(range(1, count)):
        source = index - step
        factor = lax.dynamic_index_in_dim(fwd_prod, jnp.maximum(source, 0), 0, keepdims=False)
        carry_in = jnp.where(source >= 0, received[step], 0.0) + factor * carry_in
    carry_back = jnp.zeros_like(bwd_start)
    for step in reversed(range(1, count)):
        source = index + step
        factor = lax.dynamic_index_in_dim(bwd_prod, jnp.minimum(source, count - 1), 0, keepdims=False)
        carry_back = jnp.where(source < count, received[count - step], 0.0) + factor * carry_back
    return carry_in, carry_back


def group_sum(value, axis, index, count, route):
    if count == 1:
        return value
    if count & (count - 1):
        return None
    step = 1
    while step < count:
        value = value + lax.ppermute(value, axis, route(step))
        step *= 2
    return value


def local(frames_in, in_kernel, out_kernel, decay_rate, frame_keep, out_grad):
    frame_count, row_count, col_count = frames_in.shape[:3]
    position = lax.axis_index("tm")
    blocks = lax.axis_size("tm")
    width = 2 if blocks % 2 == 0 else 1
    groups = blocks // width
    group = position // width
    upper = position % width == 1
    if width == 2:
        swap = [(i, i ^ 1) for i in range(blocks)]
        if lax.axis_size("chan") == 2:
            first = lax.axis_index("chan") == 0
            got = lax.ppermute(jnp.where(first, frames_in, out_grad), "tm", swap)
            traded = lax.ppermute(got, "chan", [(0, 1), (1, 0)])
            other_frames = jnp.where(first, got, traded)
            other_grad = jnp.where(first, traded, got)
        else:
            other_frames = lax.ppermute(frames_in, "tm", swap)
            other_grad = lax.ppermute(out_grad, "tm", swap)
        frame_blocks = [jnp.where(upper, other_frames, frames_in), jnp.where(upper, frames_in, other_frames)]
        grad_blocks = [jnp.where(upper, other_grad, out_grad), jnp.where(upper, out_grad, other_grad)]
    else:
        frame_blocks = [frames_in]
        grad_blocks = [out_grad]
    span = frame_count * width
    row_taps = row_taps_of(row_halo(frames_in), row_count)
    in_taps = prep_kernel(in_kernel, False, row_taps)
    adjoint_taps = prep_kernel(out_kernel, True, row_taps)
    values = jnp.concatenate(
        [conv_apply(block, row_halo(block), in_taps, row_taps) for block in frame_blocks]
    )
    adjoint_in = jnp.concatenate(
        [conv_apply(block, row_halo(block), adjoint_taps, row_taps) for block in grad_blocks]
    )
    input_gain = jnp.sqrt(1.0 - decay_rate * decay_rate)
    keep_padded = jnp.concatenate([frame_keep, jnp.zeros((1,), jnp.float32)])
    offset = group * span
    keep_here = lax.dynamic_slice_in_dim(keep_padded, offset, span)
    keep_next = lax.dynamic_slice_in_dim(keep_padded, offset + 1, span)
    decays = keep_here[:, None] * decay_rate[None, :]
    decays_next = keep_next[:, None] * decay_rate[None, :]

    running = None
    product = None
    local_states, products = [], []
    for t in range(span):
        fresh = input_gain * values[t]
        running = fresh if running is None else decays[t] * running + fresh
        product = decays[t] if product is None else product * decays[t]
        local_states.append(running)
        products.append(product)
    running = None
    product = None
    back_states, back_products = [None] * span, [None] * span
    for t in reversed(range(span)):
        running = adjoint_in[t] if running is None else adjoint_in[t] + decays_next[t] * running
        product = decays_next[t] if product is None else product * decays_next[t]
        back_states[t] = running
        back_products[t] = product

    all_decays = (frame_keep[:, None] * decay_rate[None, :]).reshape(groups, span, -1)
    all_next = (keep_padded[1:, None] * decay_rate[None, :]).reshape(groups, span, -1)
    fwd_prod = all_decays[:, 0]
    for t in range(1, span):
        fwd_prod = fwd_prod * all_decays[:, t]
    bwd_prod = all_next[:, span - 1]
    for t in reversed(range(span - 1)):
        bwd_prod = bwd_prod * all_next[:, t]

    def route(step, cyclic=True):
        return [
            (width * z + x, width * ((z + step) % groups if cyclic else z ^ step) + x)
            for z in range(groups)
            for x in range(width)
        ]

    carry_in, carry_back = cyclic_carries(
        local_states[-1], back_states[0], fwd_prod, bwd_prod, "tm", group, groups, route
    )

    states = jnp.stack([local_states[t] + products[t] * carry_in for t in range(span)])
    adjoints = jnp.stack([back_states[t] + back_products[t] * carry_back for t in range(span)])
    previous = jnp.concatenate([carry_in[None], states[:-1]], axis=0)
    terms = adjoints * (
        decays[:, None, None, :] * previous - decay_rate * decay_rate / input_gain * values
    )
    total_count = frame_count * blocks * row_count * lax.axis_size("rows") * col_count
    partial = jnp.sum(terms, axis=(0, 1, 2))
    summed = group_sum(partial, "tm", group, groups, lambda step: route(step, False))
    if summed is None:
        summed = lax.psum(partial, "tm") / width
    grad_decay = all_sum(summed, "rows") / math.sqrt(total_count)

    if width == 2:
        states = jnp.where(upper, states[frame_count:], states[:frame_count])
        adjoints = jnp.where(upper, adjoints[frame_count:], adjoints[:frame_count])
    state_b = states.astype(jnp.bfloat16)
    adjoint_b = adjoints.astype(jnp.bfloat16)
    mixed = chan_sum(state_b, row_halo(state_b), prep_kernel(out_kernel, False, row_taps), row_taps)
    grad_in = chan_sum(adjoint_b, row_halo(adjoint_b), prep_kernel(in_kernel, True, row_taps), row_taps)
    return (mixed, grad_in, grad_decay)


def solution(mesh):
    placed = (
        P(("grp", "tm"), "rows", None, None),
        P(None, None, None, "chan"),
        P(None, None, "chan", None),
        P("chan"),
        P("grp"),
        P(("grp", "tm"), "rows", None, None),
    )
    return jax.shard_map(
        local,
        mesh=mesh,
        in_specs=placed,
        out_specs=(
            P(("grp", "tm"), "rows", None, "chan"),
            P(("grp", "tm"), "rows", None, "chan"),
            P(("grp", "chan")),
        ),
        check_vma=False,
    )
```

```python
import math

import jax
import jax.numpy as jnp
from jax import lax
from jax.sharding import PartitionSpec as P


def row_halo(cells):
    count = lax.axis_size("rows")
    if count == 1:
        return None
    ends = count - 1
    head = cells[:, :1]
    tail = cells[:, -1:]
    top = lax.ppermute(tail, "rows", [(i, i + 1) for i in range(ends)])
    bottom = lax.ppermute(head, "rows", [(i + 1, i) for i in range(ends)])
    return top, bottom


def row_taps_of(halo, row_count):
    return (1,) if halo is None and row_count == 1 else (0, 1, 2)


def prep_kernel(kernel, transpose, row_taps):
    if transpose:
        flipped = kernel[::-1, ::-1]
        taps = jnp.stack([flipped[a] for a in row_taps])
        taps = jnp.swapaxes(taps, 2, 3)
    else:
        taps = jnp.stack([kernel[a] for a in row_taps])
    return lax.optimization_barrier(taps)


def conv_apply(cells, halo, taps, row_taps):
    frame_count, row_count, col_count, channels = cells.shape
    if len(row_taps) == 1:
        extended = jnp.pad(cells, ((0, 0), (1, 1), (0, 0), (0, 0)))
    else:
        if halo is None:
            zero = jnp.zeros_like(cells[:, :1])
            halo = (zero, zero)
        extended = jnp.concatenate([halo[0], cells, halo[1]], axis=1)
    padded = jnp.pad(extended, ((0, 0), (0, 0), (1, 1), (0, 0)))
    summed = None
    for index, row_tap in enumerate(row_taps):
        for col_tap in range(3):
            portion = padded[:, row_tap : row_tap + row_count, col_tap : col_tap + col_count, :]
            term = jnp.dot(
                portion.reshape(-1, channels),
                taps[index, col_tap],
                preferred_element_type=jnp.float32,
            )
            summed = term if summed is None else summed + term
    return summed.reshape(frame_count, row_count, col_count, -1)


def all_sum(value, axis):
    count = lax.axis_size(axis)
    if count == 1:
        return value
    if count & (count - 1) == 0:
        step = 1
        while step < count:
            value = value + lax.ppermute(value, axis, [(i, i ^ step) for i in range(count)])
            step *= 2
        return value
    return lax.psum(value, axis)


def chan_sums(jobs):
    count = lax.axis_size("chan")
    mine = lax.axis_index("chan")
    if count != 2:
        return [
            lax.psum_scatter(
                conv_apply(*job).astype(jnp.bfloat16), "chan", scatter_dimension=3, tiled=True
            )
            for job in jobs
        ]
    width = jobs[0][2].shape[3] // count
    others = []
    for cells, halo, taps, row_taps in jobs:
        other_taps = lax.dynamic_slice_in_dim(taps, (1 - mine) * width, width, axis=3)
        others.append(conv_apply(cells, halo, other_taps, row_taps).astype(jnp.bfloat16))
    got = lax.ppermute(jnp.stack(others), "chan", [(0, 1), (1, 0)])
    results = []
    for index, (cells, halo, taps, row_taps) in enumerate(jobs):
        own_taps = lax.dynamic_slice_in_dim(taps, mine * width, width, axis=3)
        own = conv_apply(cells, halo, own_taps, row_taps)
        results.append((own + got[index].astype(jnp.float32)).astype(jnp.bfloat16))
    return results


def cyclic_carries(fwd_end, bwd_start, fwd_prod, bwd_prod, axis, index, count, route):
    received = {}
    for step in range(1, count):
        message = jnp.where(index + step < count, fwd_end, bwd_start)
        received[step] = lax.ppermute(message, axis, route(step))
    carry_in = jnp.zeros_like(fwd_end)
    for step in reversed(range(1, count)):
        source = index - step
        factor = lax.dynamic_index_in_dim(fwd_prod, jnp.maximum(source, 0), 0, keepdims=False)
        carry_in = jnp.where(source >= 0, received[step], 0.0) + factor * carry_in
    carry_back = jnp.zeros_like(bwd_start)
    for step in reversed(range(1, count)):
        source = index + step
        factor = lax.dynamic_index_in_dim(bwd_prod, jnp.minimum(source, count - 1), 0, keepdims=False)
        carry_back = jnp.where(source < count, received[count - step], 0.0) + factor * carry_back
    return carry_in, carry_back


def group_sum(value, axis, index, count, route):
    if count == 1:
        return value
    if count & (count - 1):
        return None
    step = 1
    while step < count:
        value = value + lax.ppermute(value, axis, route(step))
        step *= 2
    return value


def local(frames_in, in_kernel, out_kernel, decay_rate, frame_keep, out_grad):
    frame_count, row_count, col_count = frames_in.shape[:3]
    position = lax.axis_index("tm")
    blocks = lax.axis_size("tm")
    width = 2 if blocks % 2 == 0 else 1
    groups = blocks // width
    group = position // width
    upper = position % width == 1
    if width == 2:
        swap = [(i, i ^ 1) for i in range(blocks)]
        if lax.axis_size("chan") == 2:
            first = lax.axis_index("chan") == 0
            got = lax.ppermute(jnp.where(first, frames_in, out_grad), "tm", swap)
            traded = lax.ppermute(got, "chan", [(0, 1), (1, 0)])
            other_frames = jnp.where(first, got, traded)
            other_grad = jnp.where(first, traded, got)
        else:
            other_frames = lax.ppermute(frames_in, "tm", swap)
            other_grad = lax.ppermute(out_grad, "tm", swap)
        frame_blocks = [jnp.where(upper, other_frames, frames_in), jnp.where(upper, frames_in, other_frames)]
        grad_blocks = [jnp.where(upper, other_grad, out_grad), jnp.where(upper, out_grad, other_grad)]
    else:
        frame_blocks = [frames_in]
        grad_blocks = [out_grad]
    span = frame_count * width
    row_taps = row_taps_of(row_halo(frames_in), row_count)
    in_taps = prep_kernel(in_kernel, False, row_taps)
    adjoint_taps = prep_kernel(out_kernel, True, row_taps)
    values = jnp.concatenate(
        [conv_apply(block, row_halo(block), in_taps, row_taps) for block in frame_blocks]
    )
    adjoint_in = jnp.concatenate(
        [conv_apply(block, row_halo(block), adjoint_taps, row_taps) for block in grad_blocks]
    )
    input_gain = jnp.sqrt(1.0 - decay_rate * decay_rate)
    keep_padded = jnp.concatenate([frame_keep, jnp.zeros((1,), jnp.float32)])
    offset = group * span
    keep_here = lax.dynamic_slice_in_dim(keep_padded, offset, span)
    keep_next = lax.dynamic_slice_in_dim(keep_padded, offset + 1, span)
    decays = keep_here[:, None] * decay_rate[None, :]
    decays_next = keep_next[:, None] * decay_rate[None, :]

    running = None
    product = None
    local_states, products = [], []
    for t in range(span):
        fresh = input_gain * values[t]
        running = fresh if running is None else decays[t] * running + fresh
        product = decays[t] if product is None else product * decays[t]
        local_states.append(running)
        products.append(product)
    running = None
    product = None
    back_states, back_products = [None] * span, [None] * span
    for t in reversed(range(span)):
        running = adjoint_in[t] if running is None else adjoint_in[t] + decays_next[t] * running
        product = decays_next[t] if product is None else product * decays_next[t]
        back_states[t] = running
        back_products[t] = product

    all_decays = (frame_keep[:, None] * decay_rate[None, :]).reshape(groups, span, -1)
    all_next = (keep_padded[1:, None] * decay_rate[None, :]).reshape(groups, span, -1)
    fwd_prod = all_decays[:, 0]
    for t in range(1, span):
        fwd_prod = fwd_prod * all_decays[:, t]
    bwd_prod = all_next[:, span - 1]
    for t in reversed(range(span - 1)):
        bwd_prod = bwd_prod * all_next[:, t]

    def route(step, cyclic=True):
        return [
            (width * z + x, width * ((z + step) % groups if cyclic else z ^ step) + x)
            for z in range(groups)
            for x in range(width)
        ]

    carry_in, carry_back = cyclic_carries(
        local_states[-1], back_states[0], fwd_prod, bwd_prod, "tm", group, groups, route
    )

    states = jnp.stack([local_states[t] + products[t] * carry_in for t in range(span)])
    adjoints = jnp.stack([back_states[t] + back_products[t] * carry_back for t in range(span)])
    previous = jnp.concatenate([carry_in[None], states[:-1]], axis=0)
    terms = adjoints * (
        decays[:, None, None, :] * previous - decay_rate * decay_rate / input_gain * values
    )
    total_count = frame_count * blocks * row_count * lax.axis_size("rows") * col_count
    partial = jnp.sum(terms, axis=(0, 1, 2))
    summed = group_sum(partial, "tm", group, groups, lambda step: route(step, False))
    if summed is None:
        summed = lax.psum(partial, "tm") / width
    grad_decay = all_sum(summed, "rows") / math.sqrt(total_count)

    if width == 2:
        states = jnp.where(upper, states[frame_count:], states[:frame_count])
        adjoints = jnp.where(upper, adjoints[frame_count:], adjoints[:frame_count])
    state_b = states.astype(jnp.bfloat16)
    adjoint_b = adjoints.astype(jnp.bfloat16)
    mixed, grad_in = chan_sums(
        [
            (state_b, row_halo(state_b), prep_kernel(out_kernel, False, row_taps), row_taps),
            (adjoint_b, row_halo(adjoint_b), prep_kernel(in_kernel, True, row_taps), row_taps),
        ]
    )
    return (mixed, grad_in, grad_decay)


def solution(mesh):
    placed = (
        P(("grp", "tm"), "rows", None, None),
        P(None, None, None, "chan"),
        P(None, None, "chan", None),
        P("chan"),
        P("grp"),
        P(("grp", "tm"), "rows", None, None),
    )
    return jax.shard_map(
        local,
        mesh=mesh,
        in_specs=placed,
        out_specs=(
            P(("grp", "tm"), "rows", None, "chan"),
            P(("grp", "tm"), "rows", None, "chan"),
            P(("grp", "chan")),
        ),
        check_vma=False,
    )
```

```python
import math

import jax
import jax.numpy as jnp
from jax import lax
from jax.sharding import PartitionSpec as P


def row_halo(cells):
    count = lax.axis_size("rows")
    if count == 1:
        return None
    ends = count - 1
    head = cells[:, :1]
    tail = cells[:, -1:]
    top = lax.ppermute(tail, "rows", [(i, i + 1) for i in range(ends)])
    bottom = lax.ppermute(head, "rows", [(i + 1, i) for i in range(ends)])
    return top, bottom


def row_taps_of(halo, row_count):
    return (1,) if halo is None and row_count == 1 else (0, 1, 2)


def prep_kernel(kernel, transpose, row_taps):
    if transpose:
        flipped = kernel[::-1, ::-1]
        taps = jnp.stack([flipped[a] for a in row_taps])
        taps = jnp.swapaxes(taps, 2, 3)
    else:
        taps = jnp.stack([kernel[a] for a in row_taps])
    return lax.optimization_barrier(taps)


def conv_apply(cells, halo, taps, row_taps):
    frame_count, row_count, col_count, channels = cells.shape
    if len(row_taps) == 1:
        extended = jnp.pad(cells, ((0, 0), (1, 1), (0, 0), (0, 0)))
    else:
        if halo is None:
            zero = jnp.zeros_like(cells[:, :1])
            halo = (zero, zero)
        extended = jnp.concatenate([halo[0], cells, halo[1]], axis=1)
    padded = jnp.pad(extended, ((0, 0), (0, 0), (1, 1), (0, 0)))
    summed = None
    for index, row_tap in enumerate(row_taps):
        for col_tap in range(3):
            portion = padded[:, row_tap : row_tap + row_count, col_tap : col_tap + col_count, :]
            term = jnp.dot(
                portion.reshape(-1, channels),
                taps[index, col_tap],
                preferred_element_type=jnp.float32,
            )
            summed = term if summed is None else summed + term
    return summed.reshape(frame_count, row_count, col_count, -1)


def all_sum(value, axis):
    count = lax.axis_size(axis)
    if count == 1:
        return value
    if count & (count - 1) == 0:
        step = 1
        while step < count:
            value = value + lax.ppermute(value, axis, [(i, i ^ step) for i in range(count)])
            step *= 2
        return value
    return lax.psum(value, axis)


def chan_sum(cells, halo, taps, row_taps):
    count = lax.axis_size("chan")
    mine = lax.axis_index("chan")
    width = taps.shape[3] // count
    if count != 2:
        part = conv_apply(cells, halo, taps, row_taps)
        return lax.psum_scatter(part.astype(jnp.bfloat16), "chan", scatter_dimension=3, tiled=True)
    other_taps = lax.dynamic_slice_in_dim(taps, (1 - mine) * width, width, axis=3)
    own_taps = lax.dynamic_slice_in_dim(taps, mine * width, width, axis=3)
    other = conv_apply(cells, halo, other_taps, row_taps).astype(jnp.bfloat16)
    got = lax.ppermute(other, "chan", [(0, 1), (1, 0)])
    own = conv_apply(cells, halo, own_taps, row_taps)
    return (own + got.astype(jnp.float32)).astype(jnp.bfloat16)


def cyclic_carries(fwd_end, bwd_start, fwd_prod, bwd_prod, axis, index, count, route):
    received = {}
    for step in range(1, count):
        message = jnp.where(index + step < count, fwd_end, bwd_start)
        received[step] = lax.ppermute(message, axis, route(step))
    carry_in = jnp.zeros_like(fwd_end)
    for step in reversed(range(1, count)):
        source = index - step
        factor = lax.dynamic_index_in_dim(fwd_prod, jnp.maximum(source, 0), 0, keepdims=False)
        carry_in = jnp.where(source >= 0, received[step], 0.0) + factor * carry_in
    carry_back = jnp.zeros_like(bwd_start)
    for step in reversed(range(1, count)):
        source = index + step
        factor = lax.dynamic_index_in_dim(bwd_prod, jnp.minimum(source, count - 1), 0, keepdims=False)
        carry_back = jnp.where(source < count, received[count - step], 0.0) + factor * carry_back
    return carry_in, carry_back


def group_sum(value, axis, index, count, route):
    if count == 1:
        return value
    if count & (count - 1):
        return None
    step = 1
    while step < count:
        value = value + lax.ppermute(value, axis, route(step))
        step *= 2
    return value


def local(frames_in, in_kernel, out_kernel, decay_rate, frame_keep, out_grad):
    frame_count, row_count, col_count = frames_in.shape[:3]
    position = lax.axis_index("tm")
    blocks = lax.axis_size("tm")
    width = 2 if blocks % 2 == 0 else 1
    groups = blocks // width
    group = position // width
    upper = position % width == 1
    if width == 2:
        swap = [(i, i ^ 1) for i in range(blocks)]
        if lax.axis_size("chan") == 2:
            first = lax.axis_index("chan") == 0
            both = ("tm", "chan")
            got_frames = lax.ppermute(frames_in, both, [(2 * t, 2 * (t ^ 1)) for t in range(blocks)])
            got_grad = lax.ppermute(out_grad, both, [(2 * t + 1, 2 * (t ^ 1) + 1) for t in range(blocks)])
            traded_frames = lax.ppermute(got_frames, "chan", [(0, 1)])
            traded_grad = lax.ppermute(got_grad, "chan", [(1, 0)])
            other_frames = jnp.where(first, got_frames, traded_frames)
            other_grad = jnp.where(first, traded_grad, got_grad)
        else:
            other_frames = lax.ppermute(frames_in, "tm", swap)
            other_grad = lax.ppermute(out_grad, "tm", swap)
        own_order = [frames_in, other_frames]
        grad_order = [out_grad, other_grad]
    else:
        own_order = [frames_in]
        grad_order = [out_grad]
    span = frame_count * width
    row_taps = row_taps_of(row_halo(frames_in), row_count)
    in_taps = prep_kernel(in_kernel, False, row_taps)
    adjoint_taps = prep_kernel(out_kernel, True, row_taps)

    def in_clip_order(parts):
        if width == 1:
            return parts[0]
        return jnp.concatenate(
            [jnp.where(upper, parts[1], parts[0]), jnp.where(upper, parts[0], parts[1])]
        )

    values = in_clip_order([conv_apply(b, row_halo(b), in_taps, row_taps) for b in own_order])
    adjoint_in = in_clip_order([conv_apply(b, row_halo(b), adjoint_taps, row_taps) for b in grad_order])
    input_gain = jnp.sqrt(1.0 - decay_rate * decay_rate)
    keep_padded = jnp.concatenate([frame_keep, jnp.zeros((1,), jnp.float32)])
    offset = group * span
    keep_here = lax.dynamic_slice_in_dim(keep_padded, offset, span)
    keep_next = lax.dynamic_slice_in_dim(keep_padded, offset + 1, span)
    decays = keep_here[:, None] * decay_rate[None, :]
    decays_next = keep_next[:, None] * decay_rate[None, :]

    running = None
    product = None
    local_states, products = [], []
    for t in range(span):
        fresh = input_gain * values[t]
        running = fresh if running is None else decays[t] * running + fresh
        product = decays[t] if product is None else product * decays[t]
        local_states.append(running)
        products.append(product)
    running = None
    product = None
    back_states, back_products = [None] * span, [None] * span
    for t in reversed(range(span)):
        running = adjoint_in[t] if running is None else adjoint_in[t] + decays_next[t] * running
        product = decays_next[t] if product is None else product * decays_next[t]
        back_states[t] = running
        back_products[t] = product

    all_decays = (frame_keep[:, None] * decay_rate[None, :]).reshape(groups, span, -1)
    all_next = (keep_padded[1:, None] * decay_rate[None, :]).reshape(groups, span, -1)
    fwd_prod = all_decays[:, 0]
    for t in range(1, span):
        fwd_prod = fwd_prod * all_decays[:, t]
    bwd_prod = all_next[:, span - 1]
    for t in reversed(range(span - 1)):
        bwd_prod = bwd_prod * all_next[:, t]

    def route(step, cyclic=True):
        return [
            (width * z + x, width * ((z + step) % groups if cyclic else z ^ step) + x)
            for z in range(groups)
            for x in range(width)
        ]

    carry_in, carry_back = cyclic_carries(
        local_states[-1], back_states[0], fwd_prod, bwd_prod, "tm", group, groups, route
    )

    states = jnp.stack([local_states[t] + products[t] * carry_in for t in range(span)])
    adjoints = jnp.stack([back_states[t] + back_products[t] * carry_back for t in range(span)])
    previous = jnp.concatenate([carry_in[None], states[:-1]], axis=0)
    terms = adjoints * (
        decays[:, None, None, :] * previous - decay_rate * decay_rate / input_gain * values
    )
    total_count = frame_count * blocks * row_count * lax.axis_size("rows") * col_count
    partial = jnp.sum(terms, axis=(0, 1, 2))
    summed = group_sum(partial, "tm", group, groups, lambda step: route(step, False))
    if summed is None:
        summed = lax.psum(partial, "tm") / width
    grad_decay = all_sum(summed, "rows") / math.sqrt(total_count)

    if width == 2:
        states = jnp.where(upper, states[frame_count:], states[:frame_count])
        adjoints = jnp.where(upper, adjoints[frame_count:], adjoints[:frame_count])
    state_b = states.astype(jnp.bfloat16)
    adjoint_b = adjoints.astype(jnp.bfloat16)
    mixed = chan_sum(state_b, row_halo(state_b), prep_kernel(out_kernel, False, row_taps), row_taps)
    grad_in = chan_sum(adjoint_b, row_halo(adjoint_b), prep_kernel(in_kernel, True, row_taps), row_taps)
    return (mixed, grad_in, grad_decay)


def solution(mesh):
    placed = (
        P(("grp", "tm"), "rows", None, None),
        P(None, None, None, "chan"),
        P(None, None, "chan", None),
        P("chan"),
        P("grp"),
        P(("grp", "tm"), "rows", None, None),
    )
    return jax.shard_map(
        local,
        mesh=mesh,
        in_specs=placed,
        out_specs=(
            P(("grp", "tm"), "rows", None, "chan"),
            P(("grp", "tm"), "rows", None, "chan"),
            P(("grp", "chan")),
        ),
        check_vma=False,
    )
```

```python
import math

import jax
import jax.numpy as jnp
from jax import lax
from jax.sharding import PartitionSpec as P


def row_halo(cells):
    count = lax.axis_size("rows")
    if count == 1:
        return None
    ends = count - 1
    head = cells[:, :1]
    tail = cells[:, -1:]
    top = lax.ppermute(tail, "rows", [(i, i + 1) for i in range(ends)])
    bottom = lax.ppermute(head, "rows", [(i + 1, i) for i in range(ends)])
    return top, bottom


def row_taps_of(halo, row_count):
    return (1,) if halo is None and row_count == 1 else (0, 1, 2)


def prep_kernel(kernel, transpose, row_taps):
    if transpose:
        flipped = kernel[::-1, ::-1]
        taps = jnp.stack([flipped[a] for a in row_taps])
        taps = jnp.swapaxes(taps, 2, 3)
    else:
        taps = jnp.stack([kernel[a] for a in row_taps])
    return lax.optimization_barrier(taps)


def conv_apply(cells, halo, taps, row_taps):
    frame_count, row_count, col_count, channels = cells.shape
    if len(row_taps) == 1:
        extended = jnp.pad(cells, ((0, 0), (1, 1), (0, 0), (0, 0)))
    else:
        if halo is None:
            zero = jnp.zeros_like(cells[:, :1])
            halo = (zero, zero)
        extended = jnp.concatenate([halo[0], cells, halo[1]], axis=1)
    padded = jnp.pad(extended, ((0, 0), (0, 0), (1, 1), (0, 0)))
    summed = None
    for index, row_tap in enumerate(row_taps):
        for col_tap in range(3):
            portion = padded[:, row_tap : row_tap + row_count, col_tap : col_tap + col_count, :]
            term = jnp.dot(
                portion.reshape(-1, channels),
                taps[index, col_tap],
                preferred_element_type=jnp.float32,
            )
            summed = term if summed is None else summed + term
    return summed.reshape(frame_count, row_count, col_count, -1)


def all_sum(value, axis):
    count = lax.axis_size(axis)
    if count == 1:
        return value
    if count & (count - 1) == 0:
        step = 1
        while step < count:
            value = value + lax.ppermute(value, axis, [(i, i ^ step) for i in range(count)])
            step *= 2
        return value
    return lax.psum(value, axis)


def chan_sum(cells, halo, taps, row_taps):
    count = lax.axis_size("chan")
    mine = lax.axis_index("chan")
    width = taps.shape[3] // count
    if count != 2:
        part = conv_apply(cells, halo, taps, row_taps)
        return lax.psum_scatter(part.astype(jnp.bfloat16), "chan", scatter_dimension=3, tiled=True)
    other_taps = lax.dynamic_slice_in_dim(taps, (1 - mine) * width, width, axis=3)
    own_taps = lax.dynamic_slice_in_dim(taps, mine * width, width, axis=3)
    other = conv_apply(cells, halo, other_taps, row_taps).astype(jnp.bfloat16)
    got = lax.ppermute(other, "chan", [(0, 1), (1, 0)])
    own = conv_apply(cells, halo, own_taps, row_taps)
    return (own + got.astype(jnp.float32)).astype(jnp.bfloat16)


def cyclic_carries(fwd_end, bwd_start, fwd_prod, bwd_prod, axis, index, count, route):
    received = {}
    for step in range(1, count):
        message = jnp.where(index + step < count, fwd_end, bwd_start)
        received[step] = lax.ppermute(message, axis, route(step))
    carry_in = jnp.zeros_like(fwd_end)
    for step in reversed(range(1, count)):
        source = index - step
        factor = lax.dynamic_index_in_dim(fwd_prod, jnp.maximum(source, 0), 0, keepdims=False)
        carry_in = jnp.where(source >= 0, received[step], 0.0) + factor * carry_in
    carry_back = jnp.zeros_like(bwd_start)
    for step in reversed(range(1, count)):
        source = index + step
        factor = lax.dynamic_index_in_dim(bwd_prod, jnp.minimum(source, count - 1), 0, keepdims=False)
        carry_back = jnp.where(source < count, received[count - step], 0.0) + factor * carry_back
    return carry_in, carry_back


def group_sum(value, axis, index, count, route):
    if count == 1:
        return value
    if count & (count - 1):
        return None
    step = 1
    while step < count:
        value = value + lax.ppermute(value, axis, route(step))
        step *= 2
    return value


def local(frames_in, in_kernel, out_kernel, decay_rate, frame_keep, out_grad):
    frame_count, row_count, col_count = frames_in.shape[:3]
    position = lax.axis_index("tm")
    blocks = lax.axis_size("tm")
    width = 2 if blocks % 2 == 0 else 1
    groups = blocks // width
    group = position // width
    upper = position % width == 1
    if width == 2:
        swap = [(i, i ^ 1) for i in range(blocks)]
        if lax.axis_size("chan") == 2:
            first = lax.axis_index("chan") == 0
            got = lax.ppermute(jnp.where(first, frames_in, out_grad), "tm", swap)
            traded = lax.ppermute(got, "chan", [(0, 1), (1, 0)])
            other_frames = jnp.where(first, got, traded)
            other_grad = jnp.where(first, traded, got)
        else:
            other_frames = lax.ppermute(frames_in, "tm", swap)
            other_grad = lax.ppermute(out_grad, "tm", swap)
        frame_blocks = [jnp.where(upper, other_frames, frames_in), jnp.where(upper, frames_in, other_frames)]
        grad_blocks = [jnp.where(upper, other_grad, out_grad), jnp.where(upper, out_grad, other_grad)]
    else:
        frame_blocks = [frames_in]
        grad_blocks = [out_grad]
    span = frame_count * width
    row_taps = row_taps_of(row_halo(frames_in), row_count)
    in_taps = prep_kernel(in_kernel, False, row_taps)
    adjoint_taps = prep_kernel(out_kernel, True, row_taps)
    values = jnp.concatenate(
        [conv_apply(block, row_halo(block), in_taps, row_taps) for block in frame_blocks]
    )
    adjoint_in = jnp.concatenate(
        [conv_apply(block, row_halo(block), adjoint_taps, row_taps) for block in grad_blocks]
    )
    input_gain = jnp.sqrt(1.0 - decay_rate * decay_rate)
    keep_padded = jnp.concatenate([frame_keep, jnp.zeros((1,), jnp.float32)])
    offset = group * span
    keep_here = lax.dynamic_slice_in_dim(keep_padded, offset, span)
    keep_next = lax.dynamic_slice_in_dim(keep_padded, offset + 1, span)
    decays = keep_here[:, None] * decay_rate[None, :]
    decays_next = keep_next[:, None] * decay_rate[None, :]

    running = None
    product = None
    local_states, products = [], []
    for t in range(span):
        fresh = input_gain * values[t]
        running = fresh if running is None else decays[t] * running + fresh
        product = decays[t] if product is None else product * decays[t]
        local_states.append(running)
        products.append(product)
    running = None
    product = None
    back_states, back_products = [None] * span, [None] * span
    for t in reversed(range(span)):
        running = adjoint_in[t] if running is None else adjoint_in[t] + decays_next[t] * running
        product = decays_next[t] if product is None else product * decays_next[t]
        back_states[t] = running
        back_products[t] = product

    all_decays = (frame_keep[:, None] * decay_rate[None, :]).reshape(groups, span, -1)
    all_next = (keep_padded[1:, None] * decay_rate[None, :]).reshape(groups, span, -1)
    fwd_prod = all_decays[:, 0]
    for t in range(1, span):
        fwd_prod = fwd_prod * all_decays[:, t]
    bwd_prod = all_next[:, span - 1]
    for t in reversed(range(span - 1)):
        bwd_prod = bwd_prod * all_next[:, t]

    def route(step, cyclic=True):
        return [
            (width * z + x, width * ((z + step) % groups if cyclic else z ^ step) + x)
            for z in range(groups)
            for x in range(width)
        ]

    carry_in, carry_back = cyclic_carries(
        local_states[-1], back_states[0], fwd_prod, bwd_prod, "tm", group, groups, route
    )

    value_weight = decay_rate * decay_rate / input_gain
    local_part = jnp.zeros(decay_rate.shape, jnp.float32)
    state_weight = jnp.zeros_like(carry_in)
    adjoint_weight = jnp.zeros_like(carry_in)
    cross_weight = jnp.zeros(decay_rate.shape, jnp.float32)
    for t in range(span):
        earlier = local_states[t - 1] * decays[t] if t > 0 else 0.0
        step_x = earlier - value_weight * values[t]
        step_y = decays[t] * products[t - 1] if t > 0 else decays[t]
        local_part = local_part + jnp.sum(back_states[t] * step_x, axis=(0, 1))
        state_weight = state_weight + back_states[t] * step_y
        adjoint_weight = adjoint_weight + back_products[t] * step_x
        cross_weight = cross_weight + back_products[t] * step_y

    states = jnp.stack([local_states[t] + products[t] * carry_in for t in range(span)])
    adjoints = jnp.stack([back_states[t] + back_products[t] * carry_back for t in range(span)])
    total_count = frame_count * blocks * row_count * lax.axis_size("rows") * col_count
    partial = (
        local_part
        + jnp.sum(carry_in * state_weight, axis=(0, 1))
        + jnp.sum(carry_back * adjoint_weight, axis=(0, 1))
        + cross_weight * jnp.sum(carry_back * carry_in, axis=(0, 1))
    )
    summed = group_sum(partial, "tm", group, groups, lambda step: route(step, False))
    if summed is None:
        summed = lax.psum(partial, "tm") / width
    grad_decay = all_sum(summed, "rows") / math.sqrt(total_count)

    if width == 2:
        states = jnp.where(upper, states[frame_count:], states[:frame_count])
        adjoints = jnp.where(upper, adjoints[frame_count:], adjoints[:frame_count])
    state_b = states.astype(jnp.bfloat16)
    adjoint_b = adjoints.astype(jnp.bfloat16)
    mixed = chan_sum(state_b, row_halo(state_b), prep_kernel(out_kernel, False, row_taps), row_taps)
    grad_in = chan_sum(adjoint_b, row_halo(adjoint_b), prep_kernel(in_kernel, True, row_taps), row_taps)
    return (mixed, grad_in, grad_decay)


def solution(mesh):
    placed = (
        P(("grp", "tm"), "rows", None, None),
        P(None, None, None, "chan"),
        P(None, None, "chan", None),
        P("chan"),
        P("grp"),
        P(("grp", "tm"), "rows", None, None),
    )
    return jax.shard_map(
        local,
        mesh=mesh,
        in_specs=placed,
        out_specs=(
            P(("grp", "tm"), "rows", None, "chan"),
            P(("grp", "tm"), "rows", None, "chan"),
            P(("grp", "chan")),
        ),
        check_vma=False,
    )
```

```python
import math

import jax
import jax.numpy as jnp
from jax import lax
from jax.sharding import PartitionSpec as P


def row_halo(cells):
    count = lax.axis_size("rows")
    if count == 1:
        return None
    ends = count - 1
    head = cells[:, :1]
    tail = cells[:, -1:]
    top = lax.ppermute(tail, "rows", [(i, i + 1) for i in range(ends)])
    bottom = lax.ppermute(head, "rows", [(i + 1, i) for i in range(ends)])
    return top, bottom


def row_taps_of(halo, row_count):
    return (1,) if halo is None and row_count == 1 else (0, 1, 2)


def prep_kernel(kernel, transpose, row_taps):
    if transpose:
        flipped = kernel[::-1, ::-1]
        taps = jnp.stack([flipped[a] for a in row_taps])
        taps = jnp.swapaxes(taps, 2, 3)
    else:
        taps = jnp.stack([kernel[a] for a in row_taps])
    return lax.optimization_barrier(taps)


def conv_apply(cells, halo, taps, row_taps):
    frame_count, row_count, col_count, channels = cells.shape
    if len(row_taps) == 1:
        extended = jnp.pad(cells, ((0, 0), (1, 1), (0, 0), (0, 0)))
    else:
        if halo is None:
            zero = jnp.zeros_like(cells[:, :1])
            halo = (zero, zero)
        extended = jnp.concatenate([halo[0], cells, halo[1]], axis=1)
    padded = jnp.pad(extended, ((0, 0), (0, 0), (1, 1), (0, 0)))
    summed = None
    for index, row_tap in enumerate(row_taps):
        for col_tap in range(3):
            portion = padded[:, row_tap : row_tap + row_count, col_tap : col_tap + col_count, :]
            term = jnp.dot(
                portion.reshape(-1, channels),
                taps[index, col_tap],
                preferred_element_type=jnp.float32,
            )
            summed = term if summed is None else summed + term
    return summed.reshape(frame_count, row_count, col_count, -1)


def all_sum(value, axis):
    count = lax.axis_size(axis)
    if count == 1:
        return value
    if count & (count - 1) == 0:
        step = 1
        while step < count:
            value = value + lax.ppermute(value, axis, [(i, i ^ step) for i in range(count)])
            step *= 2
        return value
    return lax.psum(value, axis)


def chan_sum(cells, halo, taps, row_taps):
    count = lax.axis_size("chan")
    mine = lax.axis_index("chan")
    width = taps.shape[3] // count
    if count != 2:
        part = conv_apply(cells, halo, taps, row_taps)
        return lax.psum_scatter(part.astype(jnp.bfloat16), "chan", scatter_dimension=3, tiled=True)
    other_taps = lax.dynamic_slice_in_dim(taps, (1 - mine) * width, width, axis=3)
    own_taps = lax.dynamic_slice_in_dim(taps, mine * width, width, axis=3)
    other = conv_apply(cells, halo, other_taps, row_taps).astype(jnp.bfloat16)
    got = lax.ppermute(other, "chan", [(0, 1), (1, 0)])
    own = conv_apply(cells, halo, own_taps, row_taps)
    return (own + got.astype(jnp.float32)).astype(jnp.bfloat16)


def cyclic_carries(fwd_end, bwd_start, fwd_prod, bwd_prod, axis, index, count, route):
    received = {}
    for step in range(1, count):
        message = jnp.where(index + step < count, fwd_end, bwd_start)
        received[step] = lax.ppermute(message, axis, route(step))
    carry_in = jnp.zeros_like(fwd_end)
    for step in reversed(range(1, count)):
        source = index - step
        factor = lax.dynamic_index_in_dim(fwd_prod, jnp.maximum(source, 0), 0, keepdims=False)
        carry_in = jnp.where(source >= 0, received[step], 0.0) + factor * carry_in
    carry_back = jnp.zeros_like(bwd_start)
    for step in reversed(range(1, count)):
        source = index + step
        factor = lax.dynamic_index_in_dim(bwd_prod, jnp.minimum(source, count - 1), 0, keepdims=False)
        carry_back = jnp.where(source < count, received[count - step], 0.0) + factor * carry_back
    return carry_in, carry_back


def group_sum(value, axis, index, count, route):
    if count == 1:
        return value
    if count & (count - 1):
        return None
    step = 1
    while step < count:
        value = value + lax.ppermute(value, axis, route(step))
        step *= 2
    return value


def local(frames_in, in_kernel, out_kernel, decay_rate, frame_keep, out_grad):
    frame_count, row_count, col_count = frames_in.shape[:3]
    position = lax.axis_index("tm")
    blocks = lax.axis_size("tm")
    width = 2 if blocks % 2 == 0 else 1
    groups = blocks // width
    group = position // width
    upper = position % width == 1
    if width == 2:
        swap = [(i, i ^ 1) for i in range(blocks)]
        if lax.axis_size("chan") == 2:
            first = lax.axis_index("chan") == 0
            outgoing = lax.cond(first, lambda: frames_in, lambda: out_grad)
            got = lax.ppermute(outgoing, "tm", swap)
            traded = lax.ppermute(got, "chan", [(0, 1), (1, 0)])
            other_frames = jnp.where(first, got, traded)
            other_grad = jnp.where(first, traded, got)
        else:
            other_frames = lax.ppermute(frames_in, "tm", swap)
            other_grad = lax.ppermute(out_grad, "tm", swap)
        frame_blocks = [jnp.where(upper, other_frames, frames_in), jnp.where(upper, frames_in, other_frames)]
        grad_blocks = [jnp.where(upper, other_grad, out_grad), jnp.where(upper, out_grad, other_grad)]
    else:
        frame_blocks = [frames_in]
        grad_blocks = [out_grad]
    span = frame_count * width
    row_taps = row_taps_of(row_halo(frames_in), row_count)
    in_taps = prep_kernel(in_kernel, False, row_taps)
    adjoint_taps = prep_kernel(out_kernel, True, row_taps)
    values = jnp.concatenate(
        [conv_apply(block, row_halo(block), in_taps, row_taps) for block in frame_blocks]
    )
    adjoint_in = jnp.concatenate(
        [conv_apply(block, row_halo(block), adjoint_taps, row_taps) for block in grad_blocks]
    )
    input_gain = jnp.sqrt(1.0 - decay_rate * decay_rate)
    keep_padded = jnp.concatenate([frame_keep, jnp.zeros((1,), jnp.float32)])
    offset = group * span
    keep_here = lax.dynamic_slice_in_dim(keep_padded, offset, span)
    keep_next = lax.dynamic_slice_in_dim(keep_padded, offset + 1, span)
    decays = keep_here[:, None] * decay_rate[None, :]
    decays_next = keep_next[:, None] * decay_rate[None, :]

    running = None
    product = None
    local_states, products = [], []
    for t in range(span):
        fresh = input_gain * values[t]
        running = fresh if running is None else decays[t] * running + fresh
        product = decays[t] if product is None else product * decays[t]
        local_states.append(running)
        products.append(product)
    running = None
    product = None
    back_states, back_products = [None] * span, [None] * span
    for t in reversed(range(span)):
        running = adjoint_in[t] if running is None else adjoint_in[t] + decays_next[t] * running
        product = decays_next[t] if product is None else product * decays_next[t]
        back_states[t] = running
        back_products[t] = product

    all_decays = (frame_keep[:, None] * decay_rate[None, :]).reshape(groups, span, -1)
    all_next = (keep_padded[1:, None] * decay_rate[None, :]).reshape(groups, span, -1)
    fwd_prod = all_decays[:, 0]
    for t in range(1, span):
        fwd_prod = fwd_prod * all_decays[:, t]
    bwd_prod = all_next[:, span - 1]
    for t in reversed(range(span - 1)):
        bwd_prod = bwd_prod * all_next[:, t]

    def route(step, cyclic=True):
        return [
            (width * z + x, width * ((z + step) % groups if cyclic else z ^ step) + x)
            for z in range(groups)
            for x in range(width)
        ]

    carry_in, carry_back = cyclic_carries(
        local_states[-1], back_states[0], fwd_prod, bwd_prod, "tm", group, groups, route
    )

    states = jnp.stack([local_states[t] + products[t] * carry_in for t in range(span)])
    adjoints = jnp.stack([back_states[t] + back_products[t] * carry_back for t in range(span)])
    previous = jnp.concatenate([carry_in[None], states[:-1]], axis=0)
    terms = adjoints * (
        decays[:, None, None, :] * previous - decay_rate * decay_rate / input_gain * values
    )
    total_count = frame_count * blocks * row_count * lax.axis_size("rows") * col_count
    partial = jnp.sum(terms, axis=(0, 1, 2))
    summed = group_sum(partial, "tm", group, groups, lambda step: route(step, False))
    if summed is None:
        summed = lax.psum(partial, "tm") / width
    grad_decay = all_sum(summed, "rows") / math.sqrt(total_count)

    if width == 2:
        states = jnp.where(upper, states[frame_count:], states[:frame_count])
        adjoints = jnp.where(upper, adjoints[frame_count:], adjoints[:frame_count])
    state_b = states.astype(jnp.bfloat16)
    adjoint_b = adjoints.astype(jnp.bfloat16)
    mixed = chan_sum(state_b, row_halo(state_b), prep_kernel(out_kernel, False, row_taps), row_taps)
    grad_in = chan_sum(adjoint_b, row_halo(adjoint_b), prep_kernel(in_kernel, True, row_taps), row_taps)
    return (mixed, grad_in, grad_decay)


def solution(mesh):
    placed = (
        P(("grp", "tm"), "rows", None, None),
        P(None, None, None, "chan"),
        P(None, None, "chan", None),
        P("chan"),
        P("grp"),
        P(("grp", "tm"), "rows", None, None),
    )
    return jax.shard_map(
        local,
        mesh=mesh,
        in_specs=placed,
        out_specs=(
            P(("grp", "tm"), "rows", None, "chan"),
            P(("grp", "tm"), "rows", None, "chan"),
            P(("grp", "chan")),
        ),
        check_vma=False,
    )
```

```python
import math

import jax
import jax.numpy as jnp
from jax import lax
from jax.sharding import PartitionSpec as P


def row_halo(cells):
    count = lax.axis_size("rows")
    if count == 1:
        return None
    ends = count - 1
    head = cells[:, :1]
    tail = cells[:, -1:]
    top = lax.ppermute(tail, "rows", [(i, i + 1) for i in range(ends)])
    bottom = lax.ppermute(head, "rows", [(i + 1, i) for i in range(ends)])
    return top, bottom


def row_taps_of(halo, row_count):
    return (1,) if halo is None and row_count == 1 else (0, 1, 2)


def prep_kernel(kernel, transpose, row_taps):
    if transpose:
        flipped = kernel[::-1, ::-1]
        taps = jnp.stack([flipped[a] for a in row_taps])
        taps = jnp.swapaxes(taps, 2, 3)
    else:
        taps = jnp.stack([kernel[a] for a in row_taps])
    return lax.optimization_barrier(taps)


def conv_apply(cells, halo, taps, row_taps):
    frame_count, row_count, col_count, channels = cells.shape
    if len(row_taps) == 1:
        extended = jnp.pad(cells, ((0, 0), (1, 1), (0, 0), (0, 0)))
    else:
        if halo is None:
            zero = jnp.zeros_like(cells[:, :1])
            halo = (zero, zero)
        extended = jnp.concatenate([halo[0], cells, halo[1]], axis=1)
    padded = jnp.pad(extended, ((0, 0), (0, 0), (1, 1), (0, 0)))
    summed = None
    for index, row_tap in enumerate(row_taps):
        for col_tap in range(3):
            portion = padded[:, row_tap : row_tap + row_count, col_tap : col_tap + col_count, :]
            term = jnp.dot(
                portion.reshape(-1, channels),
                taps[index, col_tap],
                preferred_element_type=jnp.float32,
            )
            summed = term if summed is None else summed + term
    return summed.reshape(frame_count, row_count, col_count, -1)


def all_sum(value, axis):
    count = lax.axis_size(axis)
    if count == 1:
        return value
    if count & (count - 1) == 0:
        step = 1
        while step < count:
            value = value + lax.ppermute(value, axis, [(i, i ^ step) for i in range(count)])
            step *= 2
        return value
    return lax.psum(value, axis)


def chan_sum(cells, halo, taps, row_taps):
    count = lax.axis_size("chan")
    mine = lax.axis_index("chan")
    width = taps.shape[3] // count
    if count != 2:
        part = conv_apply(cells, halo, taps, row_taps)
        return lax.psum_scatter(part.astype(jnp.bfloat16), "chan", scatter_dimension=3, tiled=True)
    other_taps = lax.dynamic_slice_in_dim(taps, (1 - mine) * width, width, axis=3)
    own_taps = lax.dynamic_slice_in_dim(taps, mine * width, width, axis=3)
    other = conv_apply(cells, halo, other_taps, row_taps).astype(jnp.bfloat16)
    got = lax.ppermute(other, "chan", [(0, 1), (1, 0)])
    own = conv_apply(cells, halo, own_taps, row_taps)
    return (own + got.astype(jnp.float32)).astype(jnp.bfloat16)


def cyclic_carries(fwd_end, bwd_start, fwd_prod, bwd_prod, axis, index, count, route):
    received = {}
    for step in range(1, count):
        message = jnp.where(index + step < count, fwd_end, bwd_start)
        received[step] = lax.ppermute(message, axis, route(step))
    carry_in = jnp.zeros_like(fwd_end)
    for step in reversed(range(1, count)):
        source = index - step
        factor = lax.dynamic_index_in_dim(fwd_prod, jnp.maximum(source, 0), 0, keepdims=False)
        carry_in = jnp.where(source >= 0, received[step], 0.0) + factor * carry_in
    carry_back = jnp.zeros_like(bwd_start)
    for step in reversed(range(1, count)):
        source = index + step
        factor = lax.dynamic_index_in_dim(bwd_prod, jnp.minimum(source, count - 1), 0, keepdims=False)
        carry_back = jnp.where(source < count, received[count - step], 0.0) + factor * carry_back
    return carry_in, carry_back


def group_sum(value, axis, index, count, route):
    if count == 1:
        return value
    got = [value] + [lax.ppermute(value, axis, route(step)) for step in range(1, count)]
    ordered = jnp.take(jnp.stack(got), (index - jnp.arange(count)) % count, axis=0)
    total = ordered[0]
    for position in range(1, count):
        total = total + ordered[position]
    return total


def local(frames_in, in_kernel, out_kernel, decay_rate, frame_keep, out_grad):
    frame_count, row_count, col_count = frames_in.shape[:3]
    position = lax.axis_index("tm")
    blocks = lax.axis_size("tm")
    width = 2 if blocks % 2 == 0 else 1
    groups = blocks // width
    group = position // width
    upper = position % width == 1
    if width == 2:
        swap = [(i, i ^ 1) for i in range(blocks)]
        if lax.axis_size("chan") == 2:
            first = lax.axis_index("chan") == 0
            got = lax.ppermute(jnp.where(first, frames_in, out_grad), "tm", swap)
            traded = lax.ppermute(got, "chan", [(0, 1), (1, 0)])
            other_frames = jnp.where(first, got, traded)
            other_grad = jnp.where(first, traded, got)
        else:
            other_frames = lax.ppermute(frames_in, "tm", swap)
            other_grad = lax.ppermute(out_grad, "tm", swap)
        frame_blocks = [jnp.where(upper, other_frames, frames_in), jnp.where(upper, frames_in, other_frames)]
        grad_blocks = [jnp.where(upper, other_grad, out_grad), jnp.where(upper, out_grad, other_grad)]
    else:
        frame_blocks = [frames_in]
        grad_blocks = [out_grad]
    span = frame_count * width
    row_taps = row_taps_of(row_halo(frames_in), row_count)
    in_taps = prep_kernel(in_kernel, False, row_taps)
    adjoint_taps = prep_kernel(out_kernel, True, row_taps)
    values = jnp.concatenate(
        [conv_apply(block, row_halo(block), in_taps, row_taps) for block in frame_blocks]
    )
    adjoint_in = jnp.concatenate(
        [conv_apply(block, row_halo(block), adjoint_taps, row_taps) for block in grad_blocks]
    )
    input_gain = jnp.sqrt(1.0 - decay_rate * decay_rate)
    keep_padded = jnp.concatenate([frame_keep, jnp.zeros((1,), jnp.float32)])
    offset = group * span
    keep_here = lax.dynamic_slice_in_dim(keep_padded, offset, span)
    keep_next = lax.dynamic_slice_in_dim(keep_padded, offset + 1, span)
    decays = keep_here[:, None] * decay_rate[None, :]
    decays_next = keep_next[:, None] * decay_rate[None, :]

    running = None
    product = None
    local_states, products = [], []
    for t in range(span):
        fresh = input_gain * values[t]
        running = fresh if running is None else decays[t] * running + fresh
        product = decays[t] if product is None else product * decays[t]
        local_states.append(running)
        products.append(product)
    running = None
    product = None
    back_states, back_products = [None] * span, [None] * span
    for t in reversed(range(span)):
        running = adjoint_in[t] if running is None else adjoint_in[t] + decays_next[t] * running
        product = decays_next[t] if product is None else product * decays_next[t]
        back_states[t] = running
        back_products[t] = product

    all_decays = (frame_keep[:, None] * decay_rate[None, :]).reshape(groups, span, -1)
    all_next = (keep_padded[1:, None] * decay_rate[None, :]).reshape(groups, span, -1)
    fwd_prod = all_decays[:, 0]
    for t in range(1, span):
        fwd_prod = fwd_prod * all_decays[:, t]
    bwd_prod = all_next[:, span - 1]
    for t in reversed(range(span - 1)):
        bwd_prod = bwd_prod * all_next[:, t]

    def route(step, cyclic=True):
        return [
            (width * z + x, width * ((z + step) % groups if cyclic else z ^ step) + x)
            for z in range(groups)
            for x in range(width)
        ]

    carry_in, carry_back = cyclic_carries(
        local_states[-1], back_states[0], fwd_prod, bwd_prod, "tm", group, groups, route
    )

    states = jnp.stack([local_states[t] + products[t] * carry_in for t in range(span)])
    adjoints = jnp.stack([back_states[t] + back_products[t] * carry_back for t in range(span)])
    previous = jnp.concatenate([carry_in[None], states[:-1]], axis=0)
    terms = adjoints * (
        decays[:, None, None, :] * previous - decay_rate * decay_rate / input_gain * values
    )
    total_count = frame_count * blocks * row_count * lax.axis_size("rows") * col_count
    partial = jnp.sum(terms, axis=(0, 1, 2))
    summed = group_sum(partial, "tm", group, groups, route)
    if summed is None:
        summed = lax.psum(partial, "tm") / width
    grad_decay = all_sum(summed, "rows") / math.sqrt(total_count)

    if width == 2:
        states = jnp.where(upper, states[frame_count:], states[:frame_count])
        adjoints = jnp.where(upper, adjoints[frame_count:], adjoints[:frame_count])
    state_b = states.astype(jnp.bfloat16)
    adjoint_b = adjoints.astype(jnp.bfloat16)
    mixed = chan_sum(state_b, row_halo(state_b), prep_kernel(out_kernel, False, row_taps), row_taps)
    grad_in = chan_sum(adjoint_b, row_halo(adjoint_b), prep_kernel(in_kernel, True, row_taps), row_taps)
    return (mixed, grad_in, grad_decay)


def solution(mesh):
    placed = (
        P(("grp", "tm"), "rows", None, None),
        P(None, None, None, "chan"),
        P(None, None, "chan", None),
        P("chan"),
        P("grp"),
        P(("grp", "tm"), "rows", None, None),
    )
    return jax.shard_map(
        local,
        mesh=mesh,
        in_specs=placed,
        out_specs=(
            P(("grp", "tm"), "rows", None, "chan"),
            P(("grp", "tm"), "rows", None, "chan"),
            P(("grp", "chan")),
        ),
        check_vma=False,
    )
```

```python
import math

import jax
import jax.numpy as jnp
from jax import lax
from jax.sharding import PartitionSpec as P


def row_halo(cells):
    count = lax.axis_size("rows")
    if count == 1:
        return None
    ends = count - 1
    head = cells[:, :1]
    tail = cells[:, -1:]
    top = lax.ppermute(tail, "rows", [(i, i + 1) for i in range(ends)])
    bottom = lax.ppermute(head, "rows", [(i + 1, i) for i in range(ends)])
    return top, bottom


def row_taps_of(halo, row_count):
    return (1,) if halo is None and row_count == 1 else (0, 1, 2)


def prep_kernel(kernel, transpose, row_taps):
    if transpose:
        flipped = kernel[::-1, ::-1]
        taps = jnp.stack([flipped[a] for a in row_taps])
        taps = jnp.swapaxes(taps, 2, 3)
    else:
        taps = jnp.stack([kernel[a] for a in row_taps])
    return lax.optimization_barrier(taps)


def conv_apply(cells, halo, taps, row_taps):
    frame_count, row_count, col_count, channels = cells.shape
    if len(row_taps) == 1:
        extended = jnp.pad(cells, ((0, 0), (1, 1), (0, 0), (0, 0)))
    else:
        if halo is None:
            zero = jnp.zeros_like(cells[:, :1])
            halo = (zero, zero)
        extended = jnp.concatenate([halo[0], cells, halo[1]], axis=1)
    padded = jnp.pad(extended, ((0, 0), (0, 0), (1, 1), (0, 0)))
    summed = None
    for index, row_tap in enumerate(row_taps):
        for col_tap in range(3):
            portion = padded[:, row_tap : row_tap + row_count, col_tap : col_tap + col_count, :]
            term = jnp.dot(
                portion.reshape(-1, channels),
                taps[index, col_tap],
                preferred_element_type=jnp.float32,
            )
            summed = term if summed is None else summed + term
    return summed.reshape(frame_count, row_count, col_count, -1)


def all_sum(value, axis):
    count = lax.axis_size(axis)
    if count == 1:
        return value
    if count & (count - 1) == 0:
        step = 1
        while step < count:
            value = value + lax.ppermute(value, axis, [(i, i ^ step) for i in range(count)])
            step *= 2
        return value
    return lax.psum(value, axis)


def chan_sums(jobs):
    count = lax.axis_size("chan")
    mine = lax.axis_index("chan")
    if count != 2:
        return [
            lax.psum_scatter(
                conv_apply(*job).astype(jnp.bfloat16), "chan", scatter_dimension=3, tiled=True
            )
            for job in jobs
        ]
    width = jobs[0][2].shape[3] // count
    others = []
    for cells, halo, taps, row_taps in jobs:
        other_taps = lax.dynamic_slice_in_dim(taps, (1 - mine) * width, width, axis=3)
        others.append(conv_apply(cells, halo, other_taps, row_taps).astype(jnp.bfloat16))
    got = lax.ppermute(jnp.stack(others), "chan", [(0, 1), (1, 0)])
    results = []
    for index, (cells, halo, taps, row_taps) in enumerate(jobs):
        own_taps = lax.dynamic_slice_in_dim(taps, mine * width, width, axis=3)
        own = conv_apply(cells, halo, own_taps, row_taps)
        results.append((own + got[index].astype(jnp.float32)).astype(jnp.bfloat16))
    return results


def cyclic_carries(fwd_end, bwd_start, fwd_prod, bwd_prod, axis, index, count, route):
    received = {}
    for step in range(1, count):
        message = jnp.where(index + step < count, fwd_end, bwd_start)
        received[step] = lax.ppermute(message, axis, route(step))
    carry_in = jnp.zeros_like(fwd_end)
    for step in reversed(range(1, count)):
        source = index - step
        factor = lax.dynamic_index_in_dim(fwd_prod, jnp.maximum(source, 0), 0, keepdims=False)
        carry_in = jnp.where(source >= 0, received[step], 0.0) + factor * carry_in
    carry_back = jnp.zeros_like(bwd_start)
    for step in reversed(range(1, count)):
        source = index + step
        factor = lax.dynamic_index_in_dim(bwd_prod, jnp.minimum(source, count - 1), 0, keepdims=False)
        carry_back = jnp.where(source < count, received[count - step], 0.0) + factor * carry_back
    return carry_in, carry_back


def group_sum(value, axis, index, count, route):
    if count == 1:
        return value
    got = [value] + [lax.ppermute(value, axis, route(step)) for step in range(1, count)]
    ordered = jnp.take(jnp.stack(got), (index - jnp.arange(count)) % count, axis=0)
    total = ordered[0]
    for position in range(1, count):
        total = total + ordered[position]
    return total


def local(frames_in, in_kernel, out_kernel, decay_rate, frame_keep, out_grad):
    frame_count, row_count, col_count = frames_in.shape[:3]
    position = lax.axis_index("tm")
    blocks = lax.axis_size("tm")
    width = 2 if blocks % 2 == 0 else 1
    groups = blocks // width
    group = position // width
    upper = position % width == 1
    if width == 2:
        swap = [(i, i ^ 1) for i in range(blocks)]
        if lax.axis_size("chan") == 2:
            first = lax.axis_index("chan") == 0
            got = lax.ppermute(jnp.where(first, frames_in, out_grad), "tm", swap)
            traded = lax.ppermute(got, "chan", [(0, 1), (1, 0)])
            other_frames = jnp.where(first, got, traded)
            other_grad = jnp.where(first, traded, got)
        else:
            other_frames = lax.ppermute(frames_in, "tm", swap)
            other_grad = lax.ppermute(out_grad, "tm", swap)
        frame_blocks = [jnp.where(upper, other_frames, frames_in), jnp.where(upper, frames_in, other_frames)]
        grad_blocks = [jnp.where(upper, other_grad, out_grad), jnp.where(upper, out_grad, other_grad)]
    else:
        frame_blocks = [frames_in]
        grad_blocks = [out_grad]
    span = frame_count * width
    row_taps = row_taps_of(row_halo(frames_in), row_count)
    in_taps = prep_kernel(in_kernel, False, row_taps)
    adjoint_taps = prep_kernel(out_kernel, True, row_taps)
    values = jnp.concatenate(
        [conv_apply(block, row_halo(block), in_taps, row_taps) for block in frame_blocks]
    )
    adjoint_in = jnp.concatenate(
        [conv_apply(block, row_halo(block), adjoint_taps, row_taps) for block in grad_blocks]
    )
    input_gain = jnp.sqrt(1.0 - decay_rate * decay_rate)
    keep_padded = jnp.concatenate([frame_keep, jnp.zeros((1,), jnp.float32)])
    offset = group * span
    keep_here = lax.dynamic_slice_in_dim(keep_padded, offset, span)
    keep_next = lax.dynamic_slice_in_dim(keep_padded, offset + 1, span)
    decays = keep_here[:, None] * decay_rate[None, :]
    decays_next = keep_next[:, None] * decay_rate[None, :]

    running = None
    product = None
    local_states, products = [], []
    for t in range(span):
        fresh = input_gain * values[t]
        running = fresh if running is None else decays[t] * running + fresh
        product = decays[t] if product is None else product * decays[t]
        local_states.append(running)
        products.append(product)
    running = None
    product = None
    back_states, back_products = [None] * span, [None] * span
    for t in reversed(range(span)):
        running = adjoint_in[t] if running is None else adjoint_in[t] + decays_next[t] * running
        product = decays_next[t] if product is None else product * decays_next[t]
        back_states[t] = running
        back_products[t] = product

    all_decays = (frame_keep[:, None] * decay_rate[None, :]).reshape(groups, span, -1)
    all_next = (keep_padded[1:, None] * decay_rate[None, :]).reshape(groups, span, -1)
    fwd_prod = all_decays[:, 0]
    for t in range(1, span):
        fwd_prod = fwd_prod * all_decays[:, t]
    bwd_prod = all_next[:, span - 1]
    for t in reversed(range(span - 1)):
        bwd_prod = bwd_prod * all_next[:, t]

    def route(step, cyclic=True):
        return [
            (width * z + x, width * ((z + step) % groups if cyclic else z ^ step) + x)
            for z in range(groups)
            for x in range(width)
        ]

    carry_in, carry_back = cyclic_carries(
        local_states[-1], back_states[0], fwd_prod, bwd_prod, "tm", group, groups, route
    )

    states = jnp.stack([local_states[t] + products[t] * carry_in for t in range(span)])
    adjoints = jnp.stack([back_states[t] + back_products[t] * carry_back for t in range(span)])
    previous = jnp.concatenate([carry_in[None], states[:-1]], axis=0)
    terms = adjoints * (
        decays[:, None, None, :] * previous - decay_rate * decay_rate / input_gain * values
    )
    total_count = frame_count * blocks * row_count * lax.axis_size("rows") * col_count
    partial = jnp.sum(terms, axis=(0, 1, 2))
    summed = group_sum(partial, "tm", group, groups, route)
    if summed is None:
        summed = lax.psum(partial, "tm") / width
    grad_decay = all_sum(summed, "rows") / math.sqrt(total_count)

    if width == 2:
        states = jnp.where(upper, states[frame_count:], states[:frame_count])
        adjoints = jnp.where(upper, adjoints[frame_count:], adjoints[:frame_count])
    state_b = states.astype(jnp.bfloat16)
    adjoint_b = adjoints.astype(jnp.bfloat16)
    mixed, grad_in = chan_sums(
        [
            (state_b, row_halo(state_b), prep_kernel(out_kernel, False, row_taps), row_taps),
            (adjoint_b, row_halo(adjoint_b), prep_kernel(in_kernel, True, row_taps), row_taps),
        ]
    )
    return (mixed, grad_in, grad_decay)


def solution(mesh):
    placed = (
        P(("grp", "tm"), "rows", None, None),
        P(None, None, None, "chan"),
        P(None, None, "chan", None),
        P("chan"),
        P("grp"),
        P(("grp", "tm"), "rows", None, None),
    )
    return jax.shard_map(
        local,
        mesh=mesh,
        in_specs=placed,
        out_specs=(
            P(("grp", "tm"), "rows", None, "chan"),
            P(("grp", "tm"), "rows", None, "chan"),
            P(("grp", "chan")),
        ),
        check_vma=False,
    )
```

```python
import math

import jax
import jax.numpy as jnp
from jax import lax
from jax.sharding import PartitionSpec as P


def row_halo(cells):
    count = lax.axis_size("rows")
    if count == 1:
        return None
    ends = count - 1
    head = cells[:, :1]
    tail = cells[:, -1:]
    top = lax.ppermute(tail, "rows", [(i, i + 1) for i in range(ends)])
    bottom = lax.ppermute(head, "rows", [(i + 1, i) for i in range(ends)])
    return top, bottom


def row_taps_of(halo, row_count):
    return (1,) if halo is None and row_count == 1 else (0, 1, 2)


def prep_kernel(kernel, transpose, row_taps):
    if transpose:
        flipped = kernel[::-1, ::-1]
        taps = jnp.stack([flipped[a] for a in row_taps])
        taps = jnp.swapaxes(taps, 2, 3)
    else:
        taps = jnp.stack([kernel[a] for a in row_taps])
    return lax.optimization_barrier(taps)


def conv_apply(cells, halo, taps, row_taps):
    frame_count, row_count, col_count, channels = cells.shape
    if len(row_taps) == 1:
        extended = jnp.pad(cells, ((0, 0), (1, 1), (0, 0), (0, 0)))
    else:
        if halo is None:
            zero = jnp.zeros_like(cells[:, :1])
            halo = (zero, zero)
        extended = jnp.concatenate([halo[0], cells, halo[1]], axis=1)
    padded = jnp.pad(extended, ((0, 0), (0, 0), (1, 1), (0, 0)))
    summed = None
    for index, row_tap in enumerate(row_taps):
        for col_tap in range(3):
            portion = padded[:, row_tap : row_tap + row_count, col_tap : col_tap + col_count, :]
            term = jnp.dot(
                portion.reshape(-1, channels),
                taps[index, col_tap],
                preferred_element_type=jnp.float32,
            )
            summed = term if summed is None else summed + term
    return summed.reshape(frame_count, row_count, col_count, -1)


def all_sum(value, axis):
    count = lax.axis_size(axis)
    if count == 1:
        return value
    if count & (count - 1) == 0:
        step = 1
        while step < count:
            value = value + lax.ppermute(value, axis, [(i, i ^ step) for i in range(count)])
            step *= 2
        return value
    return lax.psum(value, axis)


def chan_sums(jobs):
    count = lax.axis_size("chan")
    mine = lax.axis_index("chan")
    if count != 2:
        return [
            lax.psum_scatter(
                conv_apply(*job).astype(jnp.bfloat16), "chan", scatter_dimension=3, tiled=True
            )
            for job in jobs
        ]
    width = jobs[0][2].shape[3] // count
    others = []
    for cells, halo, taps, row_taps in jobs:
        other_taps = lax.dynamic_slice_in_dim(taps, (1 - mine) * width, width, axis=3)
        others.append(conv_apply(cells, halo, other_taps, row_taps).astype(jnp.bfloat16))
    got = lax.ppermute(jnp.stack(others), "chan", [(0, 1), (1, 0)])
    results = []
    for index, (cells, halo, taps, row_taps) in enumerate(jobs):
        own_taps = lax.dynamic_slice_in_dim(taps, mine * width, width, axis=3)
        own = conv_apply(cells, halo, own_taps, row_taps)
        results.append((own + got[index].astype(jnp.float32)).astype(jnp.bfloat16))
    return results


def cyclic_carries(fwd_end, bwd_start, fwd_prod, bwd_prod, axis, index, count, route):
    received = {}
    for step in range(1, count):
        message = jnp.where(index + step < count, fwd_end, bwd_start)
        received[step] = lax.ppermute(message, axis, route(step))
    carry_in = jnp.zeros_like(fwd_end)
    for step in reversed(range(1, count)):
        source = index - step
        factor = lax.dynamic_index_in_dim(fwd_prod, jnp.maximum(source, 0), 0, keepdims=False)
        carry_in = jnp.where(source >= 0, received[step], 0.0) + factor * carry_in
    carry_back = jnp.zeros_like(bwd_start)
    for step in reversed(range(1, count)):
        source = index + step
        factor = lax.dynamic_index_in_dim(bwd_prod, jnp.minimum(source, count - 1), 0, keepdims=False)
        carry_back = jnp.where(source < count, received[count - step], 0.0) + factor * carry_back
    return carry_in, carry_back


def group_sum(value, axis, index, count, route):
    if count == 1:
        return value
    got = [value] + [lax.ppermute(value, axis, route(step)) for step in range(1, count)]

    def of_group(position):
        step = (index - position) % count
        picked = got[0]
        for candidate in range(1, count):
            picked = jnp.where(step == candidate, got[candidate], picked)
        return picked

    total = of_group(0)
    for position in range(1, count):
        total = total + of_group(position)
    return total


def local(frames_in, in_kernel, out_kernel, decay_rate, frame_keep, out_grad):
    frame_count, row_count, col_count = frames_in.shape[:3]
    position = lax.axis_index("tm")
    blocks = lax.axis_size("tm")
    width = 2 if blocks % 2 == 0 else 1
    groups = blocks // width
    group = position // width
    upper = position % width == 1
    if width == 2:
        swap = [(i, i ^ 1) for i in range(blocks)]
        if lax.axis_size("chan") == 2:
            first = lax.axis_index("chan") == 0
            got = lax.ppermute(jnp.where(first, frames_in, out_grad), "tm", swap)
            traded = lax.ppermute(got, "chan", [(0, 1), (1, 0)])
            other_frames = jnp.where(first, got, traded)
            other_grad = jnp.where(first, traded, got)
        else:
            other_frames = lax.ppermute(frames_in, "tm", swap)
            other_grad = lax.ppermute(out_grad, "tm", swap)
        frame_blocks = [jnp.where(upper, other_frames, frames_in), jnp.where(upper, frames_in, other_frames)]
        grad_blocks = [jnp.where(upper, other_grad, out_grad), jnp.where(upper, out_grad, other_grad)]
    else:
        frame_blocks = [frames_in]
        grad_blocks = [out_grad]
    span = frame_count * width
    row_taps = row_taps_of(row_halo(frames_in), row_count)
    in_taps = prep_kernel(in_kernel, False, row_taps)
    adjoint_taps = prep_kernel(out_kernel, True, row_taps)
    values = jnp.concatenate(
        [conv_apply(block, row_halo(block), in_taps, row_taps) for block in frame_blocks]
    )
    adjoint_in = jnp.concatenate(
        [conv_apply(block, row_halo(block), adjoint_taps, row_taps) for block in grad_blocks]
    )
    input_gain = jnp.sqrt(1.0 - decay_rate * decay_rate)
    keep_padded = jnp.concatenate([frame_keep, jnp.zeros((1,), jnp.float32)])
    offset = group * span
    keep_here = lax.dynamic_slice_in_dim(keep_padded, offset, span)
    keep_next = lax.dynamic_slice_in_dim(keep_padded, offset + 1, span)
    decays = keep_here[:, None] * decay_rate[None, :]
    decays_next = keep_next[:, None] * decay_rate[None, :]

    running = None
    product = None
    local_states, products = [], []
    for t in range(span):
        fresh = input_gain * values[t]
        running = fresh if running is None else decays[t] * running + fresh
        product = decays[t] if product is None else product * decays[t]
        local_states.append(running)
        products.append(product)
    running = None
    product = None
    back_states, back_products = [None] * span, [None] * span
    for t in reversed(range(span)):
        running = adjoint_in[t] if running is None else adjoint_in[t] + decays_next[t] * running
        product = decays_next[t] if product is None else product * decays_next[t]
        back_states[t] = running
        back_products[t] = product

    all_decays = (frame_keep[:, None] * decay_rate[None, :]).reshape(groups, span, -1)
    all_next = (keep_padded[1:, None] * decay_rate[None, :]).reshape(groups, span, -1)
    fwd_prod = all_decays[:, 0]
    for t in range(1, span):
        fwd_prod = fwd_prod * all_decays[:, t]
    bwd_prod = all_next[:, span - 1]
    for t in reversed(range(span - 1)):
        bwd_prod = bwd_prod * all_next[:, t]

    def route(step, cyclic=True):
        return [
            (width * z + x, width * ((z + step) % groups if cyclic else z ^ step) + x)
            for z in range(groups)
            for x in range(width)
        ]

    carry_in, carry_back = cyclic_carries(
        local_states[-1], back_states[0], fwd_prod, bwd_prod, "tm", group, groups, route
    )

    states = jnp.stack([local_states[t] + products[t] * carry_in for t in range(span)])
    adjoints = jnp.stack([back_states[t] + back_products[t] * carry_back for t in range(span)])
    previous = jnp.concatenate([carry_in[None], states[:-1]], axis=0)
    terms = adjoints * (
        decays[:, None, None, :] * previous - decay_rate * decay_rate / input_gain * values
    )
    total_count = frame_count * blocks * row_count * lax.axis_size("rows") * col_count
    partial = jnp.sum(terms, axis=(0, 1, 2))
    summed = group_sum(partial, "tm", group, groups, route)
    if summed is None:
        summed = lax.psum(partial, "tm") / width
    grad_decay = all_sum(summed, "rows") / math.sqrt(total_count)

    if width == 2:
        states = jnp.where(upper, states[frame_count:], states[:frame_count])
        adjoints = jnp.where(upper, adjoints[frame_count:], adjoints[:frame_count])
    state_b = states.astype(jnp.bfloat16)
    adjoint_b = adjoints.astype(jnp.bfloat16)
    mixed, grad_in = chan_sums(
        [
            (state_b, row_halo(state_b), prep_kernel(out_kernel, False, row_taps), row_taps),
            (adjoint_b, row_halo(adjoint_b), prep_kernel(in_kernel, True, row_taps), row_taps),
        ]
    )
    return (mixed, grad_in, grad_decay)


def solution(mesh):
    placed = (
        P(("grp", "tm"), "rows", None, None),
        P(None, None, None, "chan"),
        P(None, None, "chan", None),
        P("chan"),
        P("grp"),
        P(("grp", "tm"), "rows", None, None),
    )
    return jax.shard_map(
        local,
        mesh=mesh,
        in_specs=placed,
        out_specs=(
            P(("grp", "tm"), "rows", None, "chan"),
            P(("grp", "tm"), "rows", None, "chan"),
            P(("grp", "chan")),
        ),
        check_vma=False,
    )
```

```python
import math

import jax
import jax.numpy as jnp
from jax import lax
from jax.sharding import PartitionSpec as P


def row_halo(cells):
    count = lax.axis_size("rows")
    if count == 1:
        return None
    ends = count - 1
    head = cells[:, :1]
    tail = cells[:, -1:]
    top = lax.ppermute(tail, "rows", [(i, i + 1) for i in range(ends)])
    bottom = lax.ppermute(head, "rows", [(i + 1, i) for i in range(ends)])
    return top, bottom


def row_taps_of(halo, row_count):
    return (1,) if halo is None and row_count == 1 else (0, 1, 2)


def prep_kernel(kernel, transpose, row_taps):
    if transpose:
        flipped = kernel[::-1, ::-1]
        taps = jnp.stack([flipped[a] for a in row_taps])
        taps = jnp.swapaxes(taps, 2, 3)
    else:
        taps = jnp.stack([kernel[a] for a in row_taps])
    return lax.optimization_barrier(taps)


def conv_apply(cells, halo, taps, row_taps):
    frame_count, row_count, col_count, channels = cells.shape
    if len(row_taps) == 1:
        extended = jnp.pad(cells, ((0, 0), (1, 1), (0, 0), (0, 0)))
    else:
        if halo is None:
            zero = jnp.zeros_like(cells[:, :1])
            halo = (zero, zero)
        extended = jnp.concatenate([halo[0], cells, halo[1]], axis=1)
    padded = jnp.pad(extended, ((0, 0), (0, 0), (1, 1), (0, 0)))
    summed = None
    for index, row_tap in enumerate(row_taps):
        for col_tap in range(3):
            portion = padded[:, row_tap : row_tap + row_count, col_tap : col_tap + col_count, :]
            term = jnp.dot(
                portion.reshape(-1, channels),
                taps[index, col_tap],
                preferred_element_type=jnp.float32,
            )
            summed = term if summed is None else summed + term
    return summed.reshape(frame_count, row_count, col_count, -1)


def all_sum(value, axis):
    count = lax.axis_size(axis)
    if count == 1:
        return value
    if count & (count - 1) == 0:
        step = 1
        while step < count:
            value = value + lax.ppermute(value, axis, [(i, i ^ step) for i in range(count)])
            step *= 2
        return value
    return lax.psum(value, axis)


def chan_sums(jobs):
    count = lax.axis_size("chan")
    mine = lax.axis_index("chan")
    if count != 2:
        return [
            lax.psum_scatter(
                conv_apply(*job).astype(jnp.bfloat16), "chan", scatter_dimension=3, tiled=True
            )
            for job in jobs
        ]
    width = jobs[0][2].shape[3] // count
    others = []
    for cells, halo, taps, row_taps in jobs:
        other_taps = lax.dynamic_slice_in_dim(taps, (1 - mine) * width, width, axis=3)
        others.append(conv_apply(cells, halo, other_taps, row_taps).astype(jnp.bfloat16))
    got = lax.ppermute(jnp.stack(others), "chan", [(0, 1), (1, 0)])
    results = []
    for index, (cells, halo, taps, row_taps) in enumerate(jobs):
        own_taps = lax.dynamic_slice_in_dim(taps, mine * width, width, axis=3)
        own = conv_apply(cells, halo, own_taps, row_taps)
        results.append((own + got[index].astype(jnp.float32)).astype(jnp.bfloat16))
    return results


def cyclic_carries(fwd_end, bwd_start, fwd_prod, bwd_prod, axis, index, count, route):
    received = {}
    for step in range(1, count):
        message = jnp.where(index + step < count, fwd_end, bwd_start)
        received[step] = lax.ppermute(message, axis, route(step))
    carry_in = jnp.zeros_like(fwd_end)
    for step in reversed(range(1, count)):
        source = index - step
        factor = lax.dynamic_index_in_dim(fwd_prod, jnp.maximum(source, 0), 0, keepdims=False)
        carry_in = jnp.where(source >= 0, received[step], 0.0) + factor * carry_in
    carry_back = jnp.zeros_like(bwd_start)
    for step in reversed(range(1, count)):
        source = index + step
        factor = lax.dynamic_index_in_dim(bwd_prod, jnp.minimum(source, count - 1), 0, keepdims=False)
        carry_back = jnp.where(source < count, received[count - step], 0.0) + factor * carry_back
    return carry_in, carry_back


def group_sum(value, axis, index, count, route):
    if count == 1:
        return value
    got = [value] + [lax.ppermute(value, axis, route(step)) for step in range(1, count)]

    def of_group(position):
        step = (index - position) % count
        picked = got[0]
        for candidate in range(1, count):
            picked = jnp.where(step == candidate, got[candidate], picked)
        return picked

    total = of_group(0)
    for position in range(1, count):
        total = total + of_group(position)
    return total


def local(frames_in, in_kernel, out_kernel, decay_rate, frame_keep, out_grad):
    frame_count, row_count, col_count = frames_in.shape[:3]
    position = lax.axis_index("tm")
    blocks = lax.axis_size("tm")
    width = 2 if blocks % 2 == 0 else 1
    groups = blocks // width
    group = position // width
    upper = position % width == 1
    if width == 2:
        swap = [(i, i ^ 1) for i in range(blocks)]
        if lax.axis_size("chan") == 2:
            first = lax.axis_index("chan") == 0
            outgoing = jnp.where(first, frames_in, out_grad)
            cut = frame_count // 2 if frame_count > 1 else frame_count
            pieces = [outgoing[:cut], outgoing[cut:]] if cut < frame_count else [outgoing]
            arrived = [lax.ppermute(piece, "tm", swap) for piece in pieces]
            handed = [lax.ppermute(piece, "chan", [(0, 1), (1, 0)]) for piece in arrived]
            got = jnp.concatenate(arrived)
            traded = jnp.concatenate(handed)
            other_frames = jnp.where(first, got, traded)
            other_grad = jnp.where(first, traded, got)
        else:
            other_frames = lax.ppermute(frames_in, "tm", swap)
            other_grad = lax.ppermute(out_grad, "tm", swap)
        frame_blocks = [jnp.where(upper, other_frames, frames_in), jnp.where(upper, frames_in, other_frames)]
        grad_blocks = [jnp.where(upper, other_grad, out_grad), jnp.where(upper, out_grad, other_grad)]
    else:
        frame_blocks = [frames_in]
        grad_blocks = [out_grad]
    span = frame_count * width
    row_taps = row_taps_of(row_halo(frames_in), row_count)
    in_taps = prep_kernel(in_kernel, False, row_taps)
    adjoint_taps = prep_kernel(out_kernel, True, row_taps)
    values = jnp.concatenate(
        [conv_apply(block, row_halo(block), in_taps, row_taps) for block in frame_blocks]
    )
    adjoint_in = jnp.concatenate(
        [conv_apply(block, row_halo(block), adjoint_taps, row_taps) for block in grad_blocks]
    )
    input_gain = jnp.sqrt(1.0 - decay_rate * decay_rate)
    keep_padded = jnp.concatenate([frame_keep, jnp.zeros((1,), jnp.float32)])
    offset = group * span
    keep_here = lax.dynamic_slice_in_dim(keep_padded, offset, span)
    keep_next = lax.dynamic_slice_in_dim(keep_padded, offset + 1, span)
    decays = keep_here[:, None] * decay_rate[None, :]
    decays_next = keep_next[:, None] * decay_rate[None, :]

    running = None
    product = None
    local_states, products = [], []
    for t in range(span):
        fresh = input_gain * values[t]
        running = fresh if running is None else decays[t] * running + fresh
        product = decays[t] if product is None else product * decays[t]
        local_states.append(running)
        products.append(product)
    running = None
    product = None
    back_states, back_products = [None] * span, [None] * span
    for t in reversed(range(span)):
        running = adjoint_in[t] if running is None else adjoint_in[t] + decays_next[t] * running
        product = decays_next[t] if product is None else product * decays_next[t]
        back_states[t] = running
        back_products[t] = product

    all_decays = (frame_keep[:, None] * decay_rate[None, :]).reshape(groups, span, -1)
    all_next = (keep_padded[1:, None] * decay_rate[None, :]).reshape(groups, span, -1)
    fwd_prod = all_decays[:, 0]
    for t in range(1, span):
        fwd_prod = fwd_prod * all_decays[:, t]
    bwd_prod = all_next[:, span - 1]
    for t in reversed(range(span - 1)):
        bwd_prod = bwd_prod * all_next[:, t]

    def route(step, cyclic=True):
        return [
            (width * z + x, width * ((z + step) % groups if cyclic else z ^ step) + x)
            for z in range(groups)
            for x in range(width)
        ]

    carry_in, carry_back = cyclic_carries(
        local_states[-1], back_states[0], fwd_prod, bwd_prod, "tm", group, groups, route
    )

    states = jnp.stack([local_states[t] + products[t] * carry_in for t in range(span)])
    adjoints = jnp.stack([back_states[t] + back_products[t] * carry_back for t in range(span)])
    previous = jnp.concatenate([carry_in[None], states[:-1]], axis=0)
    terms = adjoints * (
        decays[:, None, None, :] * previous - decay_rate * decay_rate / input_gain * values
    )
    total_count = frame_count * blocks * row_count * lax.axis_size("rows") * col_count
    partial = jnp.sum(terms, axis=(0, 1, 2))
    summed = group_sum(partial, "tm", group, groups, route)
    if summed is None:
        summed = lax.psum(partial, "tm") / width
    grad_decay = all_sum(summed, "rows") / math.sqrt(total_count)

    if width == 2:
        states = jnp.where(upper, states[frame_count:], states[:frame_count])
        adjoints = jnp.where(upper, adjoints[frame_count:], adjoints[:frame_count])
    state_b = states.astype(jnp.bfloat16)
    adjoint_b = adjoints.astype(jnp.bfloat16)
    mixed, grad_in = chan_sums(
        [
            (state_b, row_halo(state_b), prep_kernel(out_kernel, False, row_taps), row_taps),
            (adjoint_b, row_halo(adjoint_b), prep_kernel(in_kernel, True, row_taps), row_taps),
        ]
    )
    return (mixed, grad_in, grad_decay)


def solution(mesh):
    placed = (
        P(("grp", "tm"), "rows", None, None),
        P(None, None, None, "chan"),
        P(None, None, "chan", None),
        P("chan"),
        P("grp"),
        P(("grp", "tm"), "rows", None, None),
    )
    return jax.shard_map(
        local,
        mesh=mesh,
        in_specs=placed,
        out_specs=(
            P(("grp", "tm"), "rows", None, "chan"),
            P(("grp", "tm"), "rows", None, "chan"),
            P(("grp", "chan")),
        ),
        check_vma=False,
    )
```

```python
import math

import jax
import jax.numpy as jnp
from jax import lax
from jax.sharding import PartitionSpec as P


def row_halo(cells):
    count = lax.axis_size("rows")
    if count == 1:
        return None
    ends = count - 1
    head = cells[:, :1]
    tail = cells[:, -1:]
    top = lax.ppermute(tail, "rows", [(i, i + 1) for i in range(ends)])
    bottom = lax.ppermute(head, "rows", [(i + 1, i) for i in range(ends)])
    return top, bottom


def row_taps_of(halo, row_count):
    return (1,) if halo is None and row_count == 1 else (0, 1, 2)


def prep_kernel(kernel, transpose, row_taps):
    if transpose:
        flipped = kernel[::-1, ::-1]
        taps = jnp.stack([flipped[a] for a in row_taps])
        taps = jnp.swapaxes(taps, 2, 3)
    else:
        taps = jnp.stack([kernel[a] for a in row_taps])
    return lax.optimization_barrier(taps)


def conv_apply(cells, halo, taps, row_taps):
    frame_count, row_count, col_count, channels = cells.shape
    if len(row_taps) == 1:
        extended = jnp.pad(cells, ((0, 0), (1, 1), (0, 0), (0, 0)))
    else:
        if halo is None:
            zero = jnp.zeros_like(cells[:, :1])
            halo = (zero, zero)
        extended = jnp.concatenate([halo[0], cells, halo[1]], axis=1)
    padded = jnp.pad(extended, ((0, 0), (0, 0), (1, 1), (0, 0)))
    summed = None
    for index, row_tap in enumerate(row_taps):
        for col_tap in range(3):
            portion = padded[:, row_tap : row_tap + row_count, col_tap : col_tap + col_count, :]
            term = jnp.dot(
                portion.reshape(-1, channels),
                taps[index, col_tap],
                preferred_element_type=jnp.float32,
            )
            summed = term if summed is None else summed + term
    return summed.reshape(frame_count, row_count, col_count, -1)


def all_sum(value, axis):
    count = lax.axis_size(axis)
    if count == 1:
        return value
    if count & (count - 1) == 0:
        step = 1
        while step < count:
            value = value + lax.ppermute(value, axis, [(i, i ^ step) for i in range(count)])
            step *= 2
        return value
    return lax.psum(value, axis)


def chan_sums(jobs):
    count = lax.axis_size("chan")
    mine = lax.axis_index("chan")
    if count != 2:
        return [
            lax.psum_scatter(
                conv_apply(*job).astype(jnp.bfloat16), "chan", scatter_dimension=3, tiled=True
            )
            for job in jobs
        ]
    width = jobs[0][2].shape[3] // count
    others = []
    for cells, halo, taps, row_taps in jobs:
        other_taps = lax.dynamic_slice_in_dim(taps, (1 - mine) * width, width, axis=3)
        others.append(conv_apply(cells, halo, other_taps, row_taps).astype(jnp.bfloat16))
    got = lax.ppermute(jnp.stack(others), "chan", [(0, 1), (1, 0)])
    results = []
    for index, (cells, halo, taps, row_taps) in enumerate(jobs):
        own_taps = lax.dynamic_slice_in_dim(taps, mine * width, width, axis=3)
        own = conv_apply(cells, halo, own_taps, row_taps)
        results.append((own + got[index].astype(jnp.float32)).astype(jnp.bfloat16))
    return results


def shifted_carries(fwd_end, bwd_start, fwd_prod, bwd_prod, axis, index, count, route):
    received = {}
    for step in range(1, count):
        message = jnp.where(index + step < count, fwd_end, bwd_start)
        received[step] = lax.ppermute(message, axis, route(step))
    carry_in = jnp.zeros_like(fwd_end)
    for step in reversed(range(1, count)):
        source = index - step
        factor = lax.dynamic_index_in_dim(fwd_prod, jnp.maximum(source, 0), 0, keepdims=False)
        carry_in = jnp.where(source >= 0, received[step], 0.0) + factor * carry_in
    carry_back = jnp.zeros_like(bwd_start)
    for step in reversed(range(1, count)):
        source = index + step
        factor = lax.dynamic_index_in_dim(bwd_prod, jnp.minimum(source, count - 1), 0, keepdims=False)
        carry_back = jnp.where(source < count, received[count - step], 0.0) + factor * carry_back
    return carry_in, carry_back


def cyclic_carries(fwd_end, bwd_start, fwd_prod, bwd_prod, axis, index, count, route, partner=None):
    if partner is None or count & (count - 1):
        return shifted_carries(fwd_end, bwd_start, fwd_prod, bwd_prod, axis, index, count, route)
    received = {}
    for step in range(1, count):
        message = jnp.where((index ^ step) > index, fwd_end, bwd_start)
        received[step] = lax.ppermute(message, axis, partner(step))

    def from_group(other):
        step = index ^ other
        picked = received[1]
        for candidate in range(2, count):
            picked = jnp.where(step == candidate, received[candidate], picked)
        return picked

    carry_in = jnp.zeros_like(fwd_end)
    for other in range(count - 1):
        factor = lax.dynamic_index_in_dim(fwd_prod, other, 0, keepdims=False)
        carry_in = jnp.where(other < index, from_group(other) + factor * carry_in, carry_in)
    carry_back = jnp.zeros_like(bwd_start)
    for other in reversed(range(1, count)):
        factor = lax.dynamic_index_in_dim(bwd_prod, other, 0, keepdims=False)
        carry_back = jnp.where(other > index, from_group(other) + factor * carry_back, carry_back)
    return carry_in, carry_back


def group_sum(value, axis, index, count, route):
    if count == 1:
        return value
    got = [value] + [lax.ppermute(value, axis, route(step)) for step in range(1, count)]

    def of_group(position):
        step = (index - position) % count
        picked = got[0]
        for candidate in range(1, count):
            picked = jnp.where(step == candidate, got[candidate], picked)
        return picked

    total = of_group(0)
    for position in range(1, count):
        total = total + of_group(position)
    return total


def local(frames_in, in_kernel, out_kernel, decay_rate, frame_keep, out_grad):
    frame_count, row_count, col_count = frames_in.shape[:3]
    position = lax.axis_index("tm")
    blocks = lax.axis_size("tm")
    width = 2 if blocks % 2 == 0 else 1
    groups = blocks // width
    group = position // width
    upper = position % width == 1
    if width == 2:
        swap = [(i, i ^ 1) for i in range(blocks)]
        if lax.axis_size("chan") == 2:
            first = lax.axis_index("chan") == 0
            got = lax.ppermute(jnp.where(first, frames_in, out_grad), "tm", swap)
            traded = lax.ppermute(got, "chan", [(0, 1), (1, 0)])
            other_frames = jnp.where(first, got, traded)
            other_grad = jnp.where(first, traded, got)
        else:
            other_frames = lax.ppermute(frames_in, "tm", swap)
            other_grad = lax.ppermute(out_grad, "tm", swap)
        frame_blocks = [jnp.where(upper, other_frames, frames_in), jnp.where(upper, frames_in, other_frames)]
        grad_blocks = [jnp.where(upper, other_grad, out_grad), jnp.where(upper, out_grad, other_grad)]
    else:
        frame_blocks = [frames_in]
        grad_blocks = [out_grad]
    span = frame_count * width
    row_taps = row_taps_of(row_halo(frames_in), row_count)
    in_taps = prep_kernel(in_kernel, False, row_taps)
    adjoint_taps = prep_kernel(out_kernel, True, row_taps)
    values = jnp.concatenate(
        [conv_apply(block, row_halo(block), in_taps, row_taps) for block in frame_blocks]
    )
    adjoint_in = jnp.concatenate(
        [conv_apply(block, row_halo(block), adjoint_taps, row_taps) for block in grad_blocks]
    )
    input_gain = jnp.sqrt(1.0 - decay_rate * decay_rate)
    keep_padded = jnp.concatenate([frame_keep, jnp.zeros((1,), jnp.float32)])
    offset = group * span
    keep_here = lax.dynamic_slice_in_dim(keep_padded, offset, span)
    keep_next = lax.dynamic_slice_in_dim(keep_padded, offset + 1, span)
    decays = keep_here[:, None] * decay_rate[None, :]
    decays_next = keep_next[:, None] * decay_rate[None, :]

    running = None
    product = None
    local_states, products = [], []
    for t in range(span):
        fresh = input_gain * values[t]
        running = fresh if running is None else decays[t] * running + fresh
        product = decays[t] if product is None else product * decays[t]
        local_states.append(running)
        products.append(product)
    running = None
    product = None
    back_states, back_products = [None] * span, [None] * span
    for t in reversed(range(span)):
        running = adjoint_in[t] if running is None else adjoint_in[t] + decays_next[t] * running
        product = decays_next[t] if product is None else product * decays_next[t]
        back_states[t] = running
        back_products[t] = product

    all_decays = (frame_keep[:, None] * decay_rate[None, :]).reshape(groups, span, -1)
    all_next = (keep_padded[1:, None] * decay_rate[None, :]).reshape(groups, span, -1)
    fwd_prod = all_decays[:, 0]
    for t in range(1, span):
        fwd_prod = fwd_prod * all_decays[:, t]
    bwd_prod = all_next[:, span - 1]
    for t in reversed(range(span - 1)):
        bwd_prod = bwd_prod * all_next[:, t]

    def route(step, cyclic=True):
        return [
            (width * z + x, width * ((z + step) % groups if cyclic else z ^ step) + x)
            for z in range(groups)
            for x in range(width)
        ]

    carry_in, carry_back = cyclic_carries(
        local_states[-1], back_states[0], fwd_prod, bwd_prod, "tm", group, groups, route,
        lambda step: route(step, False),
    )

    states = jnp.stack([local_states[t] + products[t] * carry_in for t in range(span)])
    adjoints = jnp.stack([back_states[t] + back_products[t] * carry_back for t in range(span)])
    previous = jnp.concatenate([carry_in[None], states[:-1]], axis=0)
    terms = adjoints * (
        decays[:, None, None, :] * previous - decay_rate * decay_rate / input_gain * values
    )
    total_count = frame_count * blocks * row_count * lax.axis_size("rows") * col_count
    partial = jnp.sum(terms, axis=(0, 1, 2))
    summed = group_sum(partial, "tm", group, groups, route)
    if summed is None:
        summed = lax.psum(partial, "tm") / width
    grad_decay = all_sum(summed, "rows") / math.sqrt(total_count)

    if width == 2:
        states = jnp.where(upper, states[frame_count:], states[:frame_count])
        adjoints = jnp.where(upper, adjoints[frame_count:], adjoints[:frame_count])
    state_b = states.astype(jnp.bfloat16)
    adjoint_b = adjoints.astype(jnp.bfloat16)
    mixed, grad_in = chan_sums(
        [
            (state_b, row_halo(state_b), prep_kernel(out_kernel, False, row_taps), row_taps),
            (adjoint_b, row_halo(adjoint_b), prep_kernel(in_kernel, True, row_taps), row_taps),
        ]
    )
    return (mixed, grad_in, grad_decay)


def solution(mesh):
    placed = (
        P(("grp", "tm"), "rows", None, None),
        P(None, None, None, "chan"),
        P(None, None, "chan", None),
        P("chan"),
        P("grp"),
        P(("grp", "tm"), "rows", None, None),
    )
    return jax.shard_map(
        local,
        mesh=mesh,
        in_specs=placed,
        out_specs=(
            P(("grp", "tm"), "rows", None, "chan"),
            P(("grp", "tm"), "rows", None, "chan"),
            P(("grp", "chan")),
        ),
        check_vma=False,
    )
```

```python
import math

import jax
import jax.numpy as jnp
from jax import lax
from jax.sharding import PartitionSpec as P


def row_halo(cells):
    count = lax.axis_size("rows")
    if count == 1:
        return None
    ends = count - 1
    head = cells[:, :1]
    tail = cells[:, -1:]
    top = lax.ppermute(tail, "rows", [(i, i + 1) for i in range(ends)])
    bottom = lax.ppermute(head, "rows", [(i + 1, i) for i in range(ends)])
    return top, bottom


def row_taps_of(halo, row_count):
    return (1,) if halo is None and row_count == 1 else (0, 1, 2)


def prep_kernel(kernel, transpose, row_taps):
    if transpose:
        flipped = kernel[::-1, ::-1]
        taps = jnp.stack([flipped[a] for a in row_taps])
        taps = jnp.swapaxes(taps, 2, 3)
    else:
        taps = jnp.stack([kernel[a] for a in row_taps])
    return lax.optimization_barrier(taps)


def conv_apply(cells, halo, taps, row_taps):
    frame_count, row_count, col_count, channels = cells.shape
    if len(row_taps) == 1:
        extended = jnp.pad(cells, ((0, 0), (1, 1), (0, 0), (0, 0)))
    else:
        if halo is None:
            zero = jnp.zeros_like(cells[:, :1])
            halo = (zero, zero)
        extended = jnp.concatenate([halo[0], cells, halo[1]], axis=1)
    padded = jnp.pad(extended, ((0, 0), (0, 0), (1, 1), (0, 0)))
    summed = None
    for index, row_tap in enumerate(row_taps):
        for col_tap in range(3):
            portion = padded[:, row_tap : row_tap + row_count, col_tap : col_tap + col_count, :]
            term = jnp.dot(
                portion.reshape(-1, channels),
                taps[index, col_tap],
                preferred_element_type=jnp.float32,
            )
            summed = term if summed is None else summed + term
    return summed.reshape(frame_count, row_count, col_count, -1)


def all_sum(value, axis):
    count = lax.axis_size(axis)
    if count == 1:
        return value
    if count & (count - 1) == 0:
        step = 1
        while step < count:
            value = value + lax.ppermute(value, axis, [(i, i ^ step) for i in range(count)])
            step *= 2
        return value
    return lax.psum(value, axis)


def chan_sums(jobs):
    count = lax.axis_size("chan")
    mine = lax.axis_index("chan")
    if count != 2:
        return [
            lax.psum_scatter(
                conv_apply(*job).astype(jnp.bfloat16), "chan", scatter_dimension=3, tiled=True
            )
            for job in jobs
        ]
    width = jobs[0][2].shape[3] // count
    others = []
    for cells, halo, taps, row_taps in jobs:
        other_taps = lax.dynamic_slice_in_dim(taps, (1 - mine) * width, width, axis=3)
        others.append(conv_apply(cells, halo, other_taps, row_taps).astype(jnp.bfloat16))
    got = lax.ppermute(jnp.stack(others), "chan", [(0, 1), (1, 0)])
    results = []
    for index, (cells, halo, taps, row_taps) in enumerate(jobs):
        own_taps = lax.dynamic_slice_in_dim(taps, mine * width, width, axis=3)
        own = conv_apply(cells, halo, own_taps, row_taps)
        results.append((own + got[index].astype(jnp.float32)).astype(jnp.bfloat16))
    return results


def cyclic_carries(fwd_end, bwd_start, fwd_prod, bwd_prod, axis, index, count, route):
    received = {}
    for step in range(1, count):
        message = jnp.where(index + step < count, fwd_end, bwd_start)
        received[step] = lax.ppermute(message, axis, route(step))
    carry_in = jnp.zeros_like(fwd_end)
    for step in reversed(range(1, count)):
        source = index - step
        factor = lax.dynamic_index_in_dim(fwd_prod, jnp.maximum(source, 0), 0, keepdims=False)
        carry_in = jnp.where(source >= 0, received[step], 0.0) + factor * carry_in
    carry_back = jnp.zeros_like(bwd_start)
    for step in reversed(range(1, count)):
        source = index + step
        factor = lax.dynamic_index_in_dim(bwd_prod, jnp.minimum(source, count - 1), 0, keepdims=False)
        carry_back = jnp.where(source < count, received[count - step], 0.0) + factor * carry_back
    return carry_in, carry_back


def group_sum(value, axis, index, count, route):
    if count == 1:
        return value
    got = [value] + [lax.ppermute(value, axis, route(step)) for step in range(1, count)]

    def of_group(position):
        step = (index - position) % count
        picked = got[0]
        for candidate in range(1, count):
            picked = jnp.where(step == candidate, got[candidate], picked)
        return picked

    total = of_group(0)
    for position in range(1, count):
        total = total + of_group(position)
    return total


def local(frames_in, in_kernel, out_kernel, decay_rate, frame_keep, out_grad):
    frame_count, row_count, col_count = frames_in.shape[:3]
    position = lax.axis_index("tm")
    blocks = lax.axis_size("tm")
    width = 2 if blocks % 2 == 0 else 1
    groups = blocks // width
    group = position // width
    upper = position % width == 1
    if width == 2:
        swap = [(i, i ^ 1) for i in range(blocks)]
        if lax.axis_size("chan") == 2:
            first = lax.axis_index("chan") == 0
            got = lax.ppermute(jnp.where(first, frames_in, out_grad), "tm", swap)
            traded = lax.ppermute(got, "chan", [(0, 1), (1, 0)])
            other_frames = jnp.where(first, got, traded)
            other_grad = jnp.where(first, traded, got)
        else:
            other_frames = lax.ppermute(frames_in, "tm", swap)
            other_grad = lax.ppermute(out_grad, "tm", swap)
        frame_blocks = [frames_in, other_frames]
        grad_blocks = [out_grad, other_grad]
    else:
        frame_blocks = [frames_in]
        grad_blocks = [out_grad]
    span = frame_count * width
    row_taps = row_taps_of(row_halo(frames_in), row_count)
    in_taps = prep_kernel(in_kernel, False, row_taps)
    adjoint_taps = prep_kernel(out_kernel, True, row_taps)

    def in_clip_order(parts):
        if width == 1:
            return parts[0]
        return jnp.concatenate(
            [jnp.where(upper, parts[1], parts[0]), jnp.where(upper, parts[0], parts[1])]
        )

    values = in_clip_order([conv_apply(b, row_halo(b), in_taps, row_taps) for b in frame_blocks])
    adjoint_in = in_clip_order([conv_apply(b, row_halo(b), adjoint_taps, row_taps) for b in grad_blocks])
    input_gain = jnp.sqrt(1.0 - decay_rate * decay_rate)
    keep_padded = jnp.concatenate([frame_keep, jnp.zeros((1,), jnp.float32)])
    offset = group * span
    keep_here = lax.dynamic_slice_in_dim(keep_padded, offset, span)
    keep_next = lax.dynamic_slice_in_dim(keep_padded, offset + 1, span)
    decays = keep_here[:, None] * decay_rate[None, :]
    decays_next = keep_next[:, None] * decay_rate[None, :]

    running = None
    product = None
    local_states, products = [], []
    for t in range(span):
        fresh = input_gain * values[t]
        running = fresh if running is None else decays[t] * running + fresh
        product = decays[t] if product is None else product * decays[t]
        local_states.append(running)
        products.append(product)
    running = None
    product = None
    back_states, back_products = [None] * span, [None] * span
    for t in reversed(range(span)):
        running = adjoint_in[t] if running is None else adjoint_in[t] + decays_next[t] * running
        product = decays_next[t] if product is None else product * decays_next[t]
        back_states[t] = running
        back_products[t] = product

    all_decays = (frame_keep[:, None] * decay_rate[None, :]).reshape(groups, span, -1)
    all_next = (keep_padded[1:, None] * decay_rate[None, :]).reshape(groups, span, -1)
    fwd_prod = all_decays[:, 0]
    for t in range(1, span):
        fwd_prod = fwd_prod * all_decays[:, t]
    bwd_prod = all_next[:, span - 1]
    for t in reversed(range(span - 1)):
        bwd_prod = bwd_prod * all_next[:, t]

    def route(step, cyclic=True):
        return [
            (width * z + x, width * ((z + step) % groups if cyclic else z ^ step) + x)
            for z in range(groups)
            for x in range(width)
        ]

    carry_in, carry_back = cyclic_carries(
        local_states[-1], back_states[0], fwd_prod, bwd_prod, "tm", group, groups, route
    )

    states = jnp.stack([local_states[t] + products[t] * carry_in for t in range(span)])
    adjoints = jnp.stack([back_states[t] + back_products[t] * carry_back for t in range(span)])
    previous = jnp.concatenate([carry_in[None], states[:-1]], axis=0)
    terms = adjoints * (
        decays[:, None, None, :] * previous - decay_rate * decay_rate / input_gain * values
    )
    total_count = frame_count * blocks * row_count * lax.axis_size("rows") * col_count
    partial = jnp.sum(terms, axis=(0, 1, 2))
    summed = group_sum(partial, "tm", group, groups, route)
    if summed is None:
        summed = lax.psum(partial, "tm") / width
    grad_decay = all_sum(summed, "rows") / math.sqrt(total_count)

    if width == 2:
        states = jnp.where(upper, states[frame_count:], states[:frame_count])
        adjoints = jnp.where(upper, adjoints[frame_count:], adjoints[:frame_count])
    state_b = states.astype(jnp.bfloat16)
    adjoint_b = adjoints.astype(jnp.bfloat16)
    mixed, grad_in = chan_sums(
        [
            (state_b, row_halo(state_b), prep_kernel(out_kernel, False, row_taps), row_taps),
            (adjoint_b, row_halo(adjoint_b), prep_kernel(in_kernel, True, row_taps), row_taps),
        ]
    )
    return (mixed, grad_in, grad_decay)


def solution(mesh):
    placed = (
        P(("grp", "tm"), "rows", None, None),
        P(None, None, None, "chan"),
        P(None, None, "chan", None),
        P("chan"),
        P("grp"),
        P(("grp", "tm"), "rows", None, None),
    )
    return jax.shard_map(
        local,
        mesh=mesh,
        in_specs=placed,
        out_specs=(
            P(("grp", "tm"), "rows", None, "chan"),
            P(("grp", "tm"), "rows", None, "chan"),
            P(("grp", "chan")),
        ),
        check_vma=False,
    )
```

```python
import math

import jax
import jax.numpy as jnp
from jax import lax
from jax.sharding import PartitionSpec as P


def row_halo(cells):
    count = lax.axis_size("rows")
    if count == 1:
        return None
    ends = count - 1
    head = cells[:, :1]
    tail = cells[:, -1:]
    top = lax.ppermute(tail, "rows", [(i, i + 1) for i in range(ends)])
    bottom = lax.ppermute(head, "rows", [(i + 1, i) for i in range(ends)])
    return top, bottom


def row_taps_of(halo, row_count):
    return (1,) if halo is None and row_count == 1 else (0, 1, 2)


def prep_kernel(kernel, transpose, row_taps):
    if transpose:
        flipped = kernel[::-1, ::-1]
        taps = jnp.stack([flipped[a] for a in row_taps])
        taps = jnp.swapaxes(taps, 2, 3)
    else:
        taps = jnp.stack([kernel[a] for a in row_taps])
    return lax.optimization_barrier(taps)


def conv_apply(cells, halo, taps, row_taps):
    frame_count, row_count, col_count, channels = cells.shape
    if len(row_taps) == 1:
        extended = jnp.pad(cells, ((0, 0), (1, 1), (0, 0), (0, 0)))
    else:
        if halo is None:
            zero = jnp.zeros_like(cells[:, :1])
            halo = (zero, zero)
        extended = jnp.concatenate([halo[0], cells, halo[1]], axis=1)
    padded = jnp.pad(extended, ((0, 0), (0, 0), (1, 1), (0, 0)))
    summed = None
    for index, row_tap in enumerate(row_taps):
        for col_tap in range(3):
            portion = padded[:, row_tap : row_tap + row_count, col_tap : col_tap + col_count, :]
            term = jnp.dot(
                portion.reshape(-1, channels),
                taps[index, col_tap],
                preferred_element_type=jnp.float32,
            )
            summed = term if summed is None else summed + term
    return summed.reshape(frame_count, row_count, col_count, -1)


def all_sum(value, axis):
    count = lax.axis_size(axis)
    if count == 1:
        return value
    if count & (count - 1) == 0:
        step = 1
        while step < count:
            value = value + lax.ppermute(value, axis, [(i, i ^ step) for i in range(count)])
            step *= 2
        return value
    return lax.psum(value, axis)


def chan_sums(jobs):
    count = lax.axis_size("chan")
    mine = lax.axis_index("chan")
    if count != 2:
        return [
            lax.psum_scatter(
                conv_apply(*job).astype(jnp.bfloat16), "chan", scatter_dimension=3, tiled=True
            )
            for job in jobs
        ]
    width = jobs[0][2].shape[3] // count
    full = [conv_apply(*job) for job in jobs]
    others = [lax.dynamic_slice_in_dim(part, (1 - mine) * width, width, axis=3) for part in full]
    got = lax.ppermute(jnp.stack(others).astype(jnp.bfloat16), "chan", [(0, 1), (1, 0)])
    results = []
    for index, part in enumerate(full):
        own = lax.dynamic_slice_in_dim(part, mine * width, width, axis=3)
        results.append((own + got[index].astype(jnp.float32)).astype(jnp.bfloat16))
    return results


def cyclic_carries(fwd_end, bwd_start, fwd_prod, bwd_prod, axis, index, count, route):
    received = {}
    for step in range(1, count):
        message = jnp.where(index + step < count, fwd_end, bwd_start)
        received[step] = lax.ppermute(message, axis, route(step))
    carry_in = jnp.zeros_like(fwd_end)
    for step in reversed(range(1, count)):
        source = index - step
        factor = lax.dynamic_index_in_dim(fwd_prod, jnp.maximum(source, 0), 0, keepdims=False)
        carry_in = jnp.where(source >= 0, received[step], 0.0) + factor * carry_in
    carry_back = jnp.zeros_like(bwd_start)
    for step in reversed(range(1, count)):
        source = index + step
        factor = lax.dynamic_index_in_dim(bwd_prod, jnp.minimum(source, count - 1), 0, keepdims=False)
        carry_back = jnp.where(source < count, received[count - step], 0.0) + factor * carry_back
    return carry_in, carry_back


def group_sum(value, axis, index, count, route):
    if count == 1:
        return value
    got = [value] + [lax.ppermute(value, axis, route(step)) for step in range(1, count)]

    def of_group(position):
        step = (index - position) % count
        picked = got[0]
        for candidate in range(1, count):
            picked = jnp.where(step == candidate, got[candidate], picked)
        return picked

    total = of_group(0)
    for position in range(1, count):
        total = total + of_group(position)
    return total


def local(frames_in, in_kernel, out_kernel, decay_rate, frame_keep, out_grad):
    frame_count, row_count, col_count = frames_in.shape[:3]
    position = lax.axis_index("tm")
    blocks = lax.axis_size("tm")
    width = 2 if blocks % 2 == 0 else 1
    groups = blocks // width
    group = position // width
    upper = position % width == 1
    if width == 2:
        swap = [(i, i ^ 1) for i in range(blocks)]
        if lax.axis_size("chan") == 2:
            first = lax.axis_index("chan") == 0
            got = lax.ppermute(jnp.where(first, frames_in, out_grad), "tm", swap)
            traded = lax.ppermute(got, "chan", [(0, 1), (1, 0)])
            other_frames = jnp.where(first, got, traded)
            other_grad = jnp.where(first, traded, got)
        else:
            other_frames = lax.ppermute(frames_in, "tm", swap)
            other_grad = lax.ppermute(out_grad, "tm", swap)
        frame_blocks = [jnp.where(upper, other_frames, frames_in), jnp.where(upper, frames_in, other_frames)]
        grad_blocks = [jnp.where(upper, other_grad, out_grad), jnp.where(upper, out_grad, other_grad)]
    else:
        frame_blocks = [frames_in]
        grad_blocks = [out_grad]
    span = frame_count * width
    row_taps = row_taps_of(row_halo(frames_in), row_count)
    in_taps = prep_kernel(in_kernel, False, row_taps)
    adjoint_taps = prep_kernel(out_kernel, True, row_taps)
    values = jnp.concatenate(
        [conv_apply(block, row_halo(block), in_taps, row_taps) for block in frame_blocks]
    )
    adjoint_in = jnp.concatenate(
        [conv_apply(block, row_halo(block), adjoint_taps, row_taps) for block in grad_blocks]
    )
    input_gain = jnp.sqrt(1.0 - decay_rate * decay_rate)
    keep_padded = jnp.concatenate([frame_keep, jnp.zeros((1,), jnp.float32)])
    offset = group * span
    keep_here = lax.dynamic_slice_in_dim(keep_padded, offset, span)
    keep_next = lax.dynamic_slice_in_dim(keep_padded, offset + 1, span)
    decays = keep_here[:, None] * decay_rate[None, :]
    decays_next = keep_next[:, None] * decay_rate[None, :]

    running = None
    product = None
    local_states, products = [], []
    for t in range(span):
        fresh = input_gain * values[t]
        running = fresh if running is None else decays[t] * running + fresh
        product = decays[t] if product is None else product * decays[t]
        local_states.append(running)
        products.append(product)
    running = None
    product = None
    back_states, back_products = [None] * span, [None] * span
    for t in reversed(range(span)):
        running = adjoint_in[t] if running is None else adjoint_in[t] + decays_next[t] * running
        product = decays_next[t] if product is None else product * decays_next[t]
        back_states[t] = running
        back_products[t] = product

    all_decays = (frame_keep[:, None] * decay_rate[None, :]).reshape(groups, span, -1)
    all_next = (keep_padded[1:, None] * decay_rate[None, :]).reshape(groups, span, -1)
    fwd_prod = all_decays[:, 0]
    for t in range(1, span):
        fwd_prod = fwd_prod * all_decays[:, t]
    bwd_prod = all_next[:, span - 1]
    for t in reversed(range(span - 1)):
        bwd_prod = bwd_prod * all_next[:, t]

    def route(step, cyclic=True):
        return [
            (width * z + x, width * ((z + step) % groups if cyclic else z ^ step) + x)
            for z in range(groups)
            for x in range(width)
        ]

    carry_in, carry_back = cyclic_carries(
        local_states[-1], back_states[0], fwd_prod, bwd_prod, "tm", group, groups, route
    )

    states = jnp.stack([local_states[t] + products[t] * carry_in for t in range(span)])
    adjoints = jnp.stack([back_states[t] + back_products[t] * carry_back for t in range(span)])
    previous = jnp.concatenate([carry_in[None], states[:-1]], axis=0)
    terms = adjoints * (
        decays[:, None, None, :] * previous - decay_rate * decay_rate / input_gain * values
    )
    total_count = frame_count * blocks * row_count * lax.axis_size("rows") * col_count
    partial = jnp.sum(terms, axis=(0, 1, 2))
    summed = group_sum(partial, "tm", group, groups, route)
    if summed is None:
        summed = lax.psum(partial, "tm") / width
    grad_decay = all_sum(summed, "rows") / math.sqrt(total_count)

    if width == 2:
        states = jnp.where(upper, states[frame_count:], states[:frame_count])
        adjoints = jnp.where(upper, adjoints[frame_count:], adjoints[:frame_count])
    state_b = states.astype(jnp.bfloat16)
    adjoint_b = adjoints.astype(jnp.bfloat16)
    mixed, grad_in = chan_sums(
        [
            (state_b, row_halo(state_b), prep_kernel(out_kernel, False, row_taps), row_taps),
            (adjoint_b, row_halo(adjoint_b), prep_kernel(in_kernel, True, row_taps), row_taps),
        ]
    )
    return (mixed, grad_in, grad_decay)


def solution(mesh):
    placed = (
        P(("grp", "tm"), "rows", None, None),
        P(None, None, None, "chan"),
        P(None, None, "chan", None),
        P("chan"),
        P("grp"),
        P(("grp", "tm"), "rows", None, None),
    )
    return jax.shard_map(
        local,
        mesh=mesh,
        in_specs=placed,
        out_specs=(
            P(("grp", "tm"), "rows", None, "chan"),
            P(("grp", "tm"), "rows", None, "chan"),
            P(("grp", "chan")),
        ),
        check_vma=False,
    )
```
